256 devices in a mesh: seq: 64 (over x, z, core), head: 4 (over y).
Axes of the slice: x: 4, y: 4, z: 8, core: 2. Of those that a mesh axis runs over, the one named last changes fastest.
Arguments:
- acceptance_linear: bfloat16 [32768, 4096], P(('seq', 'head')), may hold values from -6 to 6
- lookup_linear: bfloat16 [32768, 4096], P(('seq', 'head')), may hold values from -6 to 6
- payload_linear: bfloat16 [32768, 4096], P(('seq', 'head')), may hold values from -6 to 6
- valve_linear: bfloat16 [32768, 4096], P(('seq', 'head')), may hold values from -6 to 6
- layer_entries: bfloat16 [32768, 4096], P(('seq', 'head')), may hold values from -6 to 6
- prompt_label: int32 [32768], replicated, may hold values from 0 to 15, never falling along the last dimension, each value on 1 to 8192 neighbouring positions
- fading_baseline: float32 [4096], replicated, may hold values from -12 to -3
- previous_mixing_share: float32 [4096], replicated, may hold values from 0.2 to 0.9
- fading_lower_map: bfloat16 [4096, 128], replicated, may hold values from -0.09375 to 0.09375
- fading_raise_map: bfloat16 [128, 4096], replicated, may hold values from -0.5 to 0.5
- diagonal_reward: float32 [4096], replicated, may hold values from -0.5 to 1
- cluster_gain_vector: float32 [4096], replicated, may hold values from 0.25 to 1.75
- cluster_mean_shift_add: float32 [4096], replicated, may hold values from -1.5 to 1.5
Outputs:
- gated: bfloat16 [32768, 4096], P(('seq', 'head'))
The draws below stay inside these ranges and needn't reach their ends.
All inputs are finite; a program needn't handle non-finite values.
Results may differ from the reference program's by a relative error of at most 0.001.
The reference program's roundings to bfloat16 on the way count: a program that leaves them out, or rounds other values in their place, can miss the bound.
Values may be sent and summed in bfloat16 or wider, within the bound.
No kernel may reach another device: no remote copies, remote signals or barrier semaphores. Data moves between devices by JAX's collectives and lax.ppermute only.
A program may use at most 192 MiB of HBM per device.

```python
import math
import jax
import jax.numpy as jnp
import numpy as np
from jax import lax

EMBEDDING_SIZE = 4096
DECAY_RANK = 128
ATTENTION_SPAN = 64
CH = 128
ATTENDER_COUNT = 64
TOKENS = 32768
LONGEST = 8192
SEGS = 16


def draw_fading_baseline(key, part):
    choose_key, fast_key, slow_key, pick_key = jax.random.split(key, 4)
    head_total = EMBEDDING_SIZE // ATTENTION_SPAN
    chooser = jax.random.uniform(choose_key, (head_total, ATTENTION_SPAN), jnp.float32)
    fast_share = 0.5
    picked = jax.random.randint(pick_key, (head_total, 1), 0, ATTENTION_SPAN)
    channel_place = jnp.arange(ATTENTION_SPAN, dtype=jnp.int32)[None, :]
    forced = channel_place == picked
    fast_channel = jnp.logical_or(chooser < fast_share, forced)
    fast_rate = jax.random.uniform(fast_key, (head_total, ATTENTION_SPAN), jnp.float32, minval=jnp.log(1.0 / 50.0), maxval=jnp.log(1.0 / 30.0))
    slow_rate = jnp.log(0.2 / LONGEST) + jax.random.uniform(slow_key, (head_total, ATTENTION_SPAN), jnp.float32, minval=-0.7, maxval=0.7)
    return jnp.where(fast_channel, fast_rate, slow_rate).reshape(EMBEDDING_SIZE).astype(jnp.float32)


def block_levels(key, extent, cuts, low, top_value):
    factor_of = 1.0
    for position, blocks in cuts:
        draws = jax.random.uniform(jax.random.fold_in(jax.random.fold_in(key, 6), position), (blocks,), jnp.float32, low / len(cuts), top_value / len(cuts))
        factor_of = factor_of * jnp.repeat(jnp.exp(draws), extent[position] // blocks).reshape((-1,) + (1,) * (len(extent) - 1 - position))
    return factor_of


def split_up(number_of, total, reach, skew):
    loads = [(1 << 20) // math.isqrt(rank ** skew) + 1 for rank in range(2, number_of + 1)]
    spare, holding = total - reach - (number_of - 1), [1] * (number_of - 1)
    while spare > 0:
        candidates = [i for i in range(number_of - 1) if holding[i] < reach]
        pool, budget = sum([loads[i] for i in candidates]), spare
        for i in candidates:
            more = min(reach - holding[i], max(1, budget * loads[i] // pool), spare)
            holding[i] = holding[i] + more
            spare = spare - more
    return np.array([reach] + holding)


def uneven(rng, number_of, total, reach, slope):
    if number_of == 2:
        one = jax.random.randint(rng, (), max(1, total - reach), min(reach, total - 1) + 1)
        return jnp.stack([one, total - one])
    lengths = jnp.asarray(split_up(number_of, total, reach, slope), jnp.int32)
    pairs = (number_of - 1) // 2
    giver, receiver = lengths[1:1 + 2 * pairs:2], lengths[2:2 + 2 * pairs:2]
    slack = jnp.minimum(giver - 1, reach - receiver)
    passed = jax.random.randint(jax.random.fold_in(rng, 1), (pairs,), 0, 1 << 20) % (slack + 1)
    lengths = lengths.at[1:1 + 2 * pairs:2].set(giver - passed).at[2:2 + 2 * pairs:2].set(receiver + passed)
    return lengths[jax.random.permutation(jax.random.fold_in(rng, 2), number_of)]


def normal_values(own_key, shape, scale, limit, shards=(), held_as=jnp.bfloat16):
    entries = scale * jax.random.normal(own_key, shape, jnp.float32)
    if shards:
        entries = entries * block_levels(own_key, shape, shards, -0.22, 0.18)
    return jnp.clip(entries, -limit, limit).astype(held_as)


def setup_inputs(seed: int = 0) -> dict:
    seeds = jax.random.split(jax.random.key(seed), 14)
    return {
        "acceptance_linear": normal_values(seeds[0], (TOKENS, EMBEDDING_SIZE), 1.0, 6.0, ((0, 256),)),
        "lookup_linear": normal_values(seeds[1], (TOKENS, EMBEDDING_SIZE), 1.0, 6.0, ((0, 256),)),
        "payload_linear": normal_values(seeds[2], (TOKENS, EMBEDDING_SIZE), 1.0, 6.0, ((0, 256),)),
        "valve_linear": normal_values(seeds[3], (TOKENS, EMBEDDING_SIZE), 1.0, 6.0, ((0, 256),)),
        "layer_entries": normal_values(seeds[4], (TOKENS, EMBEDDING_SIZE), 1.0, 6.0, ((0, 256),)),
        "prompt_label": jnp.searchsorted(jnp.cumsum(uneven(seeds[5], SEGS, TOKENS, LONGEST, 2)), jnp.arange(TOKENS), side="right").astype(jnp.int32),
        "fading_baseline": draw_fading_baseline(jax.random.fold_in(seeds[13], 71), 0),
        "previous_mixing_share": jnp.clip(jax.random.uniform(seeds[7], (EMBEDDING_SIZE,), jnp.float32, 0.2, 0.9), 0.2, 0.9),
        "fading_lower_map": normal_values(seeds[8], (EMBEDDING_SIZE, DECAY_RANK), EMBEDDING_SIZE ** -0.5, 0.09375),
        "fading_raise_map": normal_values(seeds[9], (DECAY_RANK, EMBEDDING_SIZE), 0.2, 0.5),
        "diagonal_reward": jnp.clip(jax.random.uniform(seeds[10], (EMBEDDING_SIZE,), jnp.float32, -0.5, 1.0), -0.5, 1.0),
        "cluster_gain_vector": jnp.clip(1.0 + 0.15 * jax.random.normal(seeds[11], (EMBEDDING_SIZE,), jnp.float32), 0.25, 1.75),
        "cluster_mean_shift_add": normal_values(seeds[12], (EMBEDDING_SIZE,), 0.3, 1.5, (), jnp.float32),
    }


norm_eps = 0.00064
decay_floor = -0.5
highest = lax.Precision.HIGHEST

def reference(acceptance_linear, lookup_linear, payload_linear, valve_linear, layer_entries, prompt_label, fading_baseline, previous_mixing_share, fading_lower_map, fading_raise_map, diagonal_reward, cluster_gain_vector, cluster_mean_shift_add):
    prev_rows = jnp.concatenate([jnp.zeros((1, EMBEDDING_SIZE), jnp.bfloat16), layer_entries[:-1]], axis=0)
    same_prev = jnp.concatenate([jnp.zeros((1,), bool), prompt_label[1:] == prompt_label[:-1]])
    prev_rows = jnp.where(same_prev[:, None], prev_rows, jnp.zeros_like(prev_rows))
    current = layer_entries.astype(jnp.float32)
    blended_input = (current + (prev_rows.astype(jnp.float32) - current) * previous_mixing_share).astype(jnp.bfloat16)
    decay_hidden_rows = jnp.tanh(jnp.dot(blended_input, fading_lower_map, preferred_element_type=jnp.float32)).astype(jnp.bfloat16)
    decay_score = fading_baseline + jnp.dot(decay_hidden_rows, fading_raise_map, preferred_element_type=jnp.float32)
    log_decay = jnp.maximum(-jnp.exp(decay_score), decay_floor).astype(jnp.bfloat16)
    attender_reward_table = diagonal_reward.reshape(ATTENDER_COUNT, ATTENTION_SPAN)
    causal = lax.broadcasted_iota(jnp.int32, (CH, CH), 0) > lax.broadcasted_iota(jnp.int32, (CH, CH), 1)

    def stretch_pass(carry_state, pieces):
        query_in, key_in, value_in, decay_in, seg_stretch, seg_prior = pieces
        request_vectors = query_in.astype(jnp.float32)
        lookup_vectors = key_in.astype(jnp.float32)
        payload_vectors = value_in.astype(jnp.float32)
        decays = decay_in.astype(jnp.float32)
        cumulative = jnp.cumsum(decays, axis=0)
        before = cumulative - decays
        ending = cumulative[-1]
        scaled_query = request_vectors * jnp.exp(before)
        scaled_key = lookup_vectors * jnp.exp(-cumulative)
        scores = jnp.einsum('thd,shd->hts', scaled_query, scaled_key, precision=highest)
        allowed = causal & (seg_stretch[:, None] == seg_stretch[None, :])
        scores = jnp.where(allowed[None], scores, jnp.zeros_like(scores))
        within = jnp.einsum('hts,shd->thd', scores, payload_vectors, precision=highest)
        diagonal_contribution = lax.optimization_barrier(jnp.sum(request_vectors * attender_reward_table * lookup_vectors, axis=2, keepdims=True)) * payload_vectors
        keep_first = (seg_stretch == seg_prior).astype(jnp.float32)
        carried = jnp.einsum('thd,hde->the', scaled_query * keep_first[:, None, None], carry_state, precision=highest)
        keep_last = (seg_stretch == seg_stretch[-1]).astype(jnp.float32)
        tail_keys = lookup_vectors * jnp.exp(ending[None] - cumulative) * keep_last[:, None, None]
        stretch_state = jnp.einsum('thd,the->hde', tail_keys, payload_vectors, precision=highest)
        stretch_decay = jnp.exp(ending) * (seg_stretch[-1] == seg_prior).astype(jnp.float32)
        next_state = stretch_decay[:, :, None] * carry_state + stretch_state
        return (next_state, within + diagonal_contribution + carried)
    stretch_count = TOKENS // CH
    blocked = (stretch_count, CH, ATTENDER_COUNT, ATTENTION_SPAN)
    seg_stretches = prompt_label.reshape(stretch_count, CH)
    seg_priors = jnp.concatenate([jnp.full((1,), -1, jnp.int32), seg_stretches[:-1, -1]])
    pieces = (acceptance_linear.reshape(blocked), lookup_linear.reshape(blocked), payload_linear.reshape(blocked), log_decay.reshape(blocked), seg_stretches, seg_priors)
    final_state, mixing = lax.scan(stretch_pass, jnp.zeros((ATTENDER_COUNT, ATTENTION_SPAN, ATTENTION_SPAN), jnp.float32), pieces)
    center = mixing - lax.optimization_barrier(jnp.mean(mixing, axis=3, keepdims=True))
    spread = lax.optimization_barrier(jnp.mean(center * center, axis=3, keepdims=True))
    normed = center * lax.rsqrt(spread + norm_eps) * cluster_gain_vector.reshape(ATTENDER_COUNT, ATTENTION_SPAN) + cluster_mean_shift_add.reshape(ATTENDER_COUNT, ATTENTION_SPAN)
    normed = normed.astype(jnp.bfloat16).reshape(TOKENS, EMBEDDING_SIZE)
    return (normed.astype(jnp.float32) * jax.nn.silu(valve_linear.astype(jnp.float32))).astype(jnp.bfloat16)
```

```python
import jax
import jax.numpy as jnp
from jax import lax
from jax.sharding import PartitionSpec as P

ATTENTION_SPAN = 64
CH = 128


norm_eps = 0.00064
decay_floor = -0.5
highest = lax.Precision.HIGHEST


def shifted(value, axis, by):
    size = lax.axis_size(axis)
    pairs = [(i, i + by) for i in range(size) if 0 <= i + by < size]
    return lax.ppermute(value, axis, pairs)


def earlier_segment(prompt_label, position):
    earlier = lax.dynamic_slice_in_dim(prompt_label, jnp.maximum(position - 1, 0), 1, 0)
    return jnp.where(position > 0, earlier, jnp.full_like(earlier, -1))


def local(
    acceptance_linear,
    lookup_linear,
    payload_linear,
    valve_linear,
    layer_entries,
    prompt_label,
    fading_baseline,
    previous_mixing_share,
    fading_lower_map,
    fading_raise_map,
    diagonal_reward,
    cluster_gain_vector,
    cluster_mean_shift_add,
):
    head_count = lax.axis_size("head")
    seq_index = lax.axis_index("seq")
    head_index = lax.axis_index("head")
    row_count = layer_entries.shape[0]
    block_start = (seq_index * head_count + head_index) * row_count
    own_seg = lax.dynamic_slice_in_dim(prompt_label, block_start, row_count, 0)
    prior_seg = jnp.concatenate([earlier_segment(prompt_label, block_start), own_seg[:-1]])
    edge_row = shifted(layer_entries[-1:], ("seq", "head"), 1)
    prev_rows = jnp.concatenate([edge_row, layer_entries[:-1]], axis=0)
    prev_rows = jnp.where((prior_seg == own_seg)[:, None], prev_rows, jnp.zeros_like(prev_rows))
    current = layer_entries.astype(jnp.float32)
    blended_input = (
        current + (prev_rows.astype(jnp.float32) - current) * previous_mixing_share
    ).astype(jnp.bfloat16)
    decay_hidden_rows = jnp.tanh(
        jnp.dot(blended_input, fading_lower_map, preferred_element_type=jnp.float32)
    ).astype(jnp.bfloat16)
    decay_score = fading_baseline + jnp.dot(
        decay_hidden_rows, fading_raise_map, preferred_element_type=jnp.float32
    )
    log_decay = jnp.maximum(-jnp.exp(decay_score), decay_floor).astype(jnp.bfloat16)
    query_head, key_head, value_head, decay_head = (
        lax.all_to_all(acceptance_linear, "head", split_axis=1, concat_axis=0, tiled=True),
        lax.all_to_all(lookup_linear, "head", split_axis=1, concat_axis=0, tiled=True),
        lax.all_to_all(payload_linear, "head", split_axis=1, concat_axis=0, tiled=True),
        lax.all_to_all(log_decay, "head", split_axis=1, concat_axis=0, tiled=True),
    )
    tokens = query_head.shape[0]
    partition_extent = query_head.shape[1]
    local_heads = partition_extent // ATTENTION_SPAN
    stretches = tokens // CH
    seq_start = seq_index * tokens
    seg_block = lax.dynamic_slice_in_dim(prompt_label, seq_start, tokens, 0).reshape(stretches, CH)
    seg_before = earlier_segment(prompt_label, seq_start)
    stretch_prior = jnp.concatenate([seg_before, seg_block[:-1, -1]])
    feature_start = head_index * partition_extent
    partition_reward = lax.dynamic_slice_in_dim(
        diagonal_reward, feature_start, partition_extent, 0
    ).reshape(local_heads, ATTENTION_SPAN)
    gain_local = lax.dynamic_slice_in_dim(
        cluster_gain_vector, feature_start, partition_extent, 0
    ).reshape(local_heads, ATTENTION_SPAN)
    bias_local = lax.dynamic_slice_in_dim(
        cluster_mean_shift_add, feature_start, partition_extent, 0
    ).reshape(local_heads, ATTENTION_SPAN)
    blocked = (stretches, CH, local_heads, ATTENTION_SPAN)
    request_vectors = query_head.reshape(blocked).astype(jnp.float32)
    lookup_vectors = key_head.reshape(blocked).astype(jnp.float32)
    payload_vectors = value_head.reshape(blocked).astype(jnp.float32)
    decays = decay_head.reshape(blocked).astype(jnp.float32)
    cumulative = jnp.cumsum(decays, axis=1)
    before = cumulative - decays
    ending = cumulative[:, -1]
    scaled_query = request_vectors * jnp.exp(before)
    scaled_key = lookup_vectors * jnp.exp(-cumulative)
    scores = jnp.einsum("cthd,cshd->chts", scaled_query, scaled_key, precision=highest)
    causal = lax.broadcasted_iota(jnp.int32, (CH, CH), 0) > lax.broadcasted_iota(
        jnp.int32, (CH, CH), 1
    )
    allowed = causal[None] & (seg_block[:, :, None] == seg_block[:, None, :])
    scores = jnp.where(allowed[:, None], scores, jnp.zeros_like(scores))
    within = jnp.einsum("chts,cshd->cthd", scores, payload_vectors, precision=highest)
    diagonal_contribution = (
        jnp.sum(request_vectors * partition_reward * lookup_vectors, axis=3, keepdims=True)
        * payload_vectors
    )
    keep_last = (seg_block == seg_block[:, -1:]).astype(jnp.float32)
    tail_keys = lookup_vectors * jnp.exp(ending[:, None] - cumulative) * keep_last[:, :, None, None]
    stretch_state = jnp.einsum("cthd,cthe->chde", tail_keys, payload_vectors, precision=highest)
    stretch_decay = (
        jnp.exp(ending) * (seg_block[:, -1] == stretch_prior).astype(jnp.float32)[:, None, None]
    )

    def advance(carry_state, pieces):
        factor, new_part = pieces
        return (factor[:, :, None] * carry_state + new_part, carry_state)

    zero_state = jnp.zeros((local_heads, ATTENTION_SPAN, ATTENTION_SPAN), jnp.float32)
    span_state, local_start = lax.scan(advance, zero_state, (stretch_decay, stretch_state))

    def multiply(product, factor):
        return (product * factor, product)

    span_decay, decay_before = lax.scan(
        multiply, jnp.ones((local_heads, ATTENTION_SPAN), jnp.float32), stretch_decay
    )

    seq_count = lax.axis_size("seq")
    packed = jnp.concatenate([span_state, span_decay[:, None, :]], axis=1)

    def unpack(value):
        return value[:, :ATTENTION_SPAN], value[:, ATTENTION_SPAN]

    prior_state, prior_decay = unpack(shifted(packed, "seq", 1))
    incoming, cover = prior_state, prior_decay
    reach = 1
    if seq_count > 2:
        far_state, far_decay = unpack(shifted(packed, "seq", 2))
        incoming = prior_decay[:, :, None] * far_state + prior_state
        cover = prior_decay * far_decay
        reach = 2
    while reach < seq_count - 1:
        far_state, far_decay = unpack(
            shifted(jnp.concatenate([incoming, cover[:, None, :]], axis=1), "seq", reach)
        )
        incoming = cover[:, :, None] * far_state + incoming
        cover = cover * far_decay
        reach *= 2
    start_state = local_start + decay_before[:, :, :, None] * incoming[None]
    keep_first = (seg_block == stretch_prior[:, None]).astype(jnp.float32)
    carried = jnp.einsum(
        "cthd,chde->cthe",
        scaled_query * keep_first[:, :, None, None],
        start_state,
        precision=highest,
    )
    mixing = within + diagonal_contribution + carried
    center = mixing - jnp.mean(mixing, axis=3, keepdims=True)
    spread = jnp.mean(center * center, axis=3, keepdims=True)
    normed = center * lax.rsqrt(spread + norm_eps) * gain_local + bias_local
    normed = normed.astype(jnp.bfloat16).reshape(tokens, partition_extent)
    returned = lax.all_to_all(normed, "head", split_axis=0, concat_axis=1, tiled=True)
    return (returned.astype(jnp.float32) * jax.nn.silu(valve_linear.astype(jnp.float32))).astype(
        jnp.bfloat16
    )


def solution(mesh):
    return jax.shard_map(
        local,
        mesh=mesh,
        in_specs=(
            P(("seq", "head"), None),
            P(("seq", "head"), None),
            P(("seq", "head"), None),
            P(("seq", "head"), None),
            P(("seq", "head"), None),
            P(),
            P(),
            P(),
            P(),
            P(),
            P(),
            P(),
            P(),
        ),
        out_specs=P(("seq", "head"), None),
        check_vma=False,
    )
```

```python
import jax
import jax.numpy as jnp
from jax import lax
from jax.sharding import PartitionSpec as P

ATTENTION_SPAN = 64
CH = 128


norm_eps = 0.00064
decay_floor = -0.5
highest = lax.Precision.HIGHEST


def shifted(value, axis, by):
    size = lax.axis_size(axis)
    pairs = [(i, i + by) for i in range(size) if 0 <= i + by < size]
    return lax.ppermute(value, axis, pairs)


def earlier_segment(prompt_label, position):
    earlier = lax.dynamic_slice_in_dim(prompt_label, jnp.maximum(position - 1, 0), 1, 0)
    return jnp.where(position > 0, earlier, jnp.full_like(earlier, -1))


def local(
    acceptance_linear,
    lookup_linear,
    payload_linear,
    valve_linear,
    layer_entries,
    prompt_label,
    fading_baseline,
    previous_mixing_share,
    fading_lower_map,
    fading_raise_map,
    diagonal_reward,
    cluster_gain_vector,
    cluster_mean_shift_add,
):
    head_count = lax.axis_size("head")
    seq_index = lax.axis_index("seq")
    head_index = lax.axis_index("head")
    row_count = layer_entries.shape[0]
    block_start = (seq_index * head_count + head_index) * row_count
    own_seg = lax.dynamic_slice_in_dim(prompt_label, block_start, row_count, 0)
    prior_seg = jnp.concatenate([earlier_segment(prompt_label, block_start), own_seg[:-1]])
    edge_row = shifted(layer_entries[-1:], ("seq", "head"), 1)
    prev_rows = jnp.concatenate([edge_row, layer_entries[:-1]], axis=0)
    prev_rows = jnp.where((prior_seg == own_seg)[:, None], prev_rows, jnp.zeros_like(prev_rows))
    current = layer_entries.astype(jnp.float32)
    blended_input = (
        current + (prev_rows.astype(jnp.float32) - current) * previous_mixing_share
    ).astype(jnp.bfloat16)
    decay_hidden_rows = jnp.tanh(
        jnp.dot(blended_input, fading_lower_map, preferred_element_type=jnp.float32)
    ).astype(jnp.bfloat16)
    decay_score = fading_baseline + jnp.dot(
        decay_hidden_rows, fading_raise_map, preferred_element_type=jnp.float32
    )
    log_decay = jnp.maximum(-jnp.exp(decay_score), decay_floor).astype(jnp.bfloat16)
    query_head, key_head, value_head, decay_head = (
        lax.all_to_all(acceptance_linear, "head", split_axis=1, concat_axis=0, tiled=True),
        lax.all_to_all(lookup_linear, "head", split_axis=1, concat_axis=0, tiled=True),
        lax.all_to_all(payload_linear, "head", split_axis=1, concat_axis=0, tiled=True),
        lax.all_to_all(log_decay, "head", split_axis=1, concat_axis=0, tiled=True),
    )
    tokens = query_head.shape[0]
    partition_extent = query_head.shape[1]
    local_heads = partition_extent // ATTENTION_SPAN
    stretches = tokens // CH
    seq_start = seq_index * tokens
    seg_block = lax.dynamic_slice_in_dim(prompt_label, seq_start, tokens, 0).reshape(stretches, CH)
    seg_before = earlier_segment(prompt_label, seq_start)
    stretch_prior = jnp.concatenate([seg_before, seg_block[:-1, -1]])
    feature_start = head_index * partition_extent
    partition_reward = lax.dynamic_slice_in_dim(
        diagonal_reward, feature_start, partition_extent, 0
    ).reshape(local_heads, ATTENTION_SPAN)
    gain_local = lax.dynamic_slice_in_dim(
        cluster_gain_vector, feature_start, partition_extent, 0
    ).reshape(local_heads, ATTENTION_SPAN)
    bias_local = lax.dynamic_slice_in_dim(
        cluster_mean_shift_add, feature_start, partition_extent, 0
    ).reshape(local_heads, ATTENTION_SPAN)
    blocked = (stretches, CH, local_heads, ATTENTION_SPAN)
    request_vectors = query_head.reshape(blocked).astype(jnp.float32)
    lookup_vectors = key_head.reshape(blocked).astype(jnp.float32)
    payload_vectors = value_head.reshape(blocked).astype(jnp.float32)
    decays = decay_head.reshape(blocked).astype(jnp.float32)
    cumulative = jnp.cumsum(decays, axis=1)
    before = cumulative - decays
    ending = cumulative[:, -1]
    scaled_query = request_vectors * jnp.exp(before)
    scaled_key = lookup_vectors * jnp.exp(-cumulative)
    scores = jnp.einsum("cthd,cshd->chts", scaled_query, scaled_key, precision=highest)
    causal = lax.broadcasted_iota(jnp.int32, (CH, CH), 0) > lax.broadcasted_iota(
        jnp.int32, (CH, CH), 1
    )
    allowed = causal[None] & (seg_block[:, :, None] == seg_block[:, None, :])
    scores = jnp.where(allowed[:, None], scores, jnp.zeros_like(scores))
    within = jnp.einsum("chts,cshd->cthd", scores, payload_vectors, precision=highest)
    diagonal_contribution = (
        jnp.sum(request_vectors * partition_reward * lookup_vectors, axis=3, keepdims=True)
        * payload_vectors
    )
    keep_last = (seg_block == seg_block[:, -1:]).astype(jnp.float32)
    tail_keys = lookup_vectors * jnp.exp(ending[:, None] - cumulative) * keep_last[:, :, None, None]
    stretch_state = jnp.einsum("cthd,cthe->chde", tail_keys, payload_vectors, precision=highest)
    stretch_decay = (
        jnp.exp(ending) * (seg_block[:, -1] == stretch_prior).astype(jnp.float32)[:, None, None]
    )

    def advance(carry_state, pieces):
        factor, new_part = pieces
        return (factor[:, :, None] * carry_state + new_part, carry_state)

    zero_state = jnp.zeros((local_heads, ATTENTION_SPAN, ATTENTION_SPAN), jnp.float32)
    span_state, local_start = lax.scan(advance, zero_state, (stretch_decay, stretch_state))

    def multiply(product, factor):
        return (product * factor, product)

    span_decay, decay_before = lax.scan(
        multiply, jnp.ones((local_heads, ATTENTION_SPAN), jnp.float32), stretch_decay
    )

    seq_count = lax.axis_size("seq")

    def compose(later, earlier):
        later_state, later_decay = later
        earlier_state, earlier_decay = earlier
        return (
            later_decay[:, :, None] * earlier_state + later_state,
            later_decay * earlier_decay,
        )

    own = (span_state, span_decay)
    reach = min(4, seq_count - 1)
    pieces = [shifted(own, "seq", by) for by in range(1, reach + 1)]
    gathered = pieces[-1]
    for piece in pieces[-2::-1]:
        gathered = compose(piece, gathered)
    while reach < seq_count - 1:
        steps = [reach * j for j in range(1, 4) if reach * j < seq_count]
        pieces = [shifted(gathered, "seq", by) for by in steps]
        combined = pieces[-1]
        for piece in pieces[-2::-1]:
            combined = compose(piece, combined)
        gathered = compose(gathered, combined)
        reach *= 4
    incoming = gathered[0]
    start_state = local_start + decay_before[:, :, :, None] * incoming[None]
    keep_first = (seg_block == stretch_prior[:, None]).astype(jnp.float32)
    carried = jnp.einsum(
        "cthd,chde->cthe",
        scaled_query * keep_first[:, :, None, None],
        start_state,
        precision=highest,
    )
    mixing = within + diagonal_contribution + carried
    center = mixing - jnp.mean(mixing, axis=3, keepdims=True)
    spread = jnp.mean(center * center, axis=3, keepdims=True)
    normed = center * lax.rsqrt(spread + norm_eps) * gain_local + bias_local
    normed = normed.astype(jnp.bfloat16).reshape(tokens, partition_extent)
    returned = lax.all_to_all(normed, "head", split_axis=0, concat_axis=1, tiled=True)
    return (returned.astype(jnp.float32) * jax.nn.silu(valve_linear.astype(jnp.float32))).astype(
        jnp.bfloat16
    )


def solution(mesh):
    return jax.shard_map(
        local,
        mesh=mesh,
        in_specs=(
            P(("seq", "head"), None),
            P(("seq", "head"), None),
            P(("seq", "head"), None),
            P(("seq", "head"), None),
            P(("seq", "head"), None),
            P(),
            P(),
            P(),
            P(),
            P(),
            P(),
            P(),
            P(),
        ),
        out_specs=P(("seq", "head"), None),
        check_vma=False,
    )
```

```python
import jax
import jax.numpy as jnp
from jax import lax
from jax.sharding import PartitionSpec as P

ATTENTION_SPAN = 64
CH = 128


norm_eps = 0.00064
decay_floor = -0.5
highest = lax.Precision.HIGHEST


def shifted(value, axis, by):
    size = lax.axis_size(axis)
    pairs = [(i, i + by) for i in range(size) if 0 <= i + by < size]
    return lax.ppermute(value, axis, pairs)


def earlier_segment(prompt_label, position):
    earlier = lax.dynamic_slice_in_dim(prompt_label, jnp.maximum(position - 1, 0), 1, 0)
    return jnp.where(position > 0, earlier, jnp.full_like(earlier, -1))


def local(
    acceptance_linear,
    lookup_linear,
    payload_linear,
    valve_linear,
    layer_entries,
    prompt_label,
    fading_baseline,
    previous_mixing_share,
    fading_lower_map,
    fading_raise_map,
    diagonal_reward,
    cluster_gain_vector,
    cluster_mean_shift_add,
):
    head_count = lax.axis_size("head")
    seq_index = lax.axis_index(("x", "z", "core"))
    head_index = lax.axis_index("head")
    row_count = layer_entries.shape[0]
    block_start = (seq_index * head_count + head_index) * row_count
    own_seg = lax.dynamic_slice_in_dim(prompt_label, block_start, row_count, 0)
    prior_seg = jnp.concatenate([earlier_segment(prompt_label, block_start), own_seg[:-1]])
    edge_row = shifted(layer_entries[-1:], ("x", "z", "core", "head"), 1)
    prev_rows = jnp.concatenate([edge_row, layer_entries[:-1]], axis=0)
    prev_rows = jnp.where((prior_seg == own_seg)[:, None], prev_rows, jnp.zeros_like(prev_rows))
    current = layer_entries.astype(jnp.float32)
    blended_input = (
        current + (prev_rows.astype(jnp.float32) - current) * previous_mixing_share
    ).astype(jnp.bfloat16)
    decay_hidden_rows = jnp.tanh(
        jnp.dot(blended_input, fading_lower_map, preferred_element_type=jnp.float32)
    ).astype(jnp.bfloat16)
    decay_score = fading_baseline + jnp.dot(
        decay_hidden_rows, fading_raise_map, preferred_element_type=jnp.float32
    )
    log_decay = jnp.maximum(-jnp.exp(decay_score), decay_floor).astype(jnp.bfloat16)
    query_head, key_head, value_head, decay_head = (
        lax.all_to_all(acceptance_linear, "head", split_axis=1, concat_axis=0, tiled=True),
        lax.all_to_all(lookup_linear, "head", split_axis=1, concat_axis=0, tiled=True),
        lax.all_to_all(payload_linear, "head", split_axis=1, concat_axis=0, tiled=True),
        lax.all_to_all(log_decay, "head", split_axis=1, concat_axis=0, tiled=True),
    )
    tokens = query_head.shape[0]
    partition_extent = query_head.shape[1]
    local_heads = partition_extent // ATTENTION_SPAN
    stretches = tokens // CH
    seq_start = seq_index * tokens
    seg_block = lax.dynamic_slice_in_dim(prompt_label, seq_start, tokens, 0).reshape(stretches, CH)
    seg_before = earlier_segment(prompt_label, seq_start)
    stretch_prior = jnp.concatenate([seg_before, seg_block[:-1, -1]])
    feature_start = head_index * partition_extent
    partition_reward = lax.dynamic_slice_in_dim(
        diagonal_reward, feature_start, partition_extent, 0
    ).reshape(local_heads, ATTENTION_SPAN)
    gain_local = lax.dynamic_slice_in_dim(
        cluster_gain_vector, feature_start, partition_extent, 0
    ).reshape(local_heads, ATTENTION_SPAN)
    bias_local = lax.dynamic_slice_in_dim(
        cluster_mean_shift_add, feature_start, partition_extent, 0
    ).reshape(local_heads, ATTENTION_SPAN)
    blocked = (stretches, CH, local_heads, ATTENTION_SPAN)
    request_vectors = query_head.reshape(blocked).astype(jnp.float32)
    lookup_vectors = key_head.reshape(blocked).astype(jnp.float32)
    payload_vectors = value_head.reshape(blocked).astype(jnp.float32)
    decays = decay_head.reshape(blocked).astype(jnp.float32)
    cumulative = jnp.cumsum(decays, axis=1)
    before = cumulative - decays
    ending = cumulative[:, -1]
    scaled_query = request_vectors * jnp.exp(before)
    scaled_key = lookup_vectors * jnp.exp(-cumulative)
    scores = jnp.einsum("cthd,cshd->chts", scaled_query, scaled_key, precision=highest)
    causal = lax.broadcasted_iota(jnp.int32, (CH, CH), 0) > lax.broadcasted_iota(
        jnp.int32, (CH, CH), 1
    )
    allowed = causal[None] & (seg_block[:, :, None] == seg_block[:, None, :])
    scores = jnp.where(allowed[:, None], scores, jnp.zeros_like(scores))
    within = jnp.einsum("chts,cshd->cthd", scores, payload_vectors, precision=highest)
    diagonal_contribution = (
        jnp.sum(request_vectors * partition_reward * lookup_vectors, axis=3, keepdims=True)
        * payload_vectors
    )
    keep_last = (seg_block == seg_block[:, -1:]).astype(jnp.float32)
    tail_keys = lookup_vectors * jnp.exp(ending[:, None] - cumulative) * keep_last[:, :, None, None]
    stretch_state = jnp.einsum("cthd,cthe->chde", tail_keys, payload_vectors, precision=highest)
    stretch_decay = (
        jnp.exp(ending) * (seg_block[:, -1] == stretch_prior).astype(jnp.float32)[:, None, None]
    )

    def advance(carry_state, pieces):
        factor, new_part = pieces
        return (factor[:, :, None] * carry_state + new_part, carry_state)

    zero_state = jnp.zeros((local_heads, ATTENTION_SPAN, ATTENTION_SPAN), jnp.float32)
    span_state, local_start = lax.scan(advance, zero_state, (stretch_decay, stretch_state))

    def multiply(product, factor):
        return (product * factor, product)

    span_decay, decay_before = lax.scan(
        multiply, jnp.ones((local_heads, ATTENTION_SPAN), jnp.float32), stretch_decay
    )

    def fold(gathered, position):
        count = gathered.shape[0]
        prefix_state = jnp.zeros_like(gathered[0, :, :ATTENTION_SPAN])
        prefix_decay = jnp.ones_like(gathered[0, :, ATTENTION_SPAN])
        total_state, total_decay = prefix_state, prefix_decay
        for k in range(count):
            part_decay = gathered[k, :, ATTENTION_SPAN]
            part_state = gathered[k, :, :ATTENTION_SPAN]
            take = k < position
            prefix_state = jnp.where(
                take, part_decay[:, :, None] * prefix_state + part_state, prefix_state
            )
            prefix_decay = jnp.where(take, part_decay * prefix_decay, prefix_decay)
            total_state = part_decay[:, :, None] * total_state + part_state
            total_decay = part_decay * total_decay
        return (
            jnp.concatenate([prefix_state, prefix_decay[:, None, :]], axis=1),
            jnp.concatenate([total_state, total_decay[:, None, :]], axis=1),
        )

    own = jnp.concatenate([span_state, span_decay[:, None, :]], axis=1)
    core_prefix, core_total = fold(lax.all_gather(own, "core"), lax.axis_index("core"))
    z_prefix, z_total = fold(lax.all_gather(core_total, "z"), lax.axis_index("z"))
    x_prefix, _ = fold(lax.all_gather(z_total, "x"), lax.axis_index("x"))
    incoming = x_prefix[:, :ATTENTION_SPAN]
    for level in (z_prefix, core_prefix):
        incoming = level[:, ATTENTION_SPAN][:, :, None] * incoming + level[:, :ATTENTION_SPAN]
    start_state = local_start + decay_before[:, :, :, None] * incoming[None]
    keep_first = (seg_block == stretch_prior[:, None]).astype(jnp.float32)
    carried = jnp.einsum(
        "cthd,chde->cthe",
        scaled_query * keep_first[:, :, None, None],
        start_state,
        precision=highest,
    )
    mixing = within + diagonal_contribution + carried
    center = mixing - jnp.mean(mixing, axis=3, keepdims=True)
    spread = jnp.mean(center * center, axis=3, keepdims=True)
    normed = center * lax.rsqrt(spread + norm_eps) * gain_local + bias_local
    normed = normed.astype(jnp.bfloat16).reshape(tokens, partition_extent)
    returned = lax.all_to_all(normed, "head", split_axis=0, concat_axis=1, tiled=True)
    return (returned.astype(jnp.float32) * jax.nn.silu(valve_linear.astype(jnp.float32))).astype(
        jnp.bfloat16
    )


def solution(mesh):
    seq_count, head_count = mesh.devices.shape
    core_count = 2
    z_count = min(8, seq_count // core_count)
    fine_mesh = jax.sharding.Mesh(
        mesh.devices.reshape(seq_count // (z_count * core_count), z_count, core_count, head_count),
        ("x", "z", "core", "head"),
    )
    return jax.shard_map(
        local,
        mesh=fine_mesh,
        in_specs=(
            P(("x", "z", "core", "head"), None),
            P(("x", "z", "core", "head"), None),
            P(("x", "z", "core", "head"), None),
            P(("x", "z", "core", "head"), None),
            P(("x", "z", "core", "head"), None),
            P(),
            P(),
            P(),
            P(),
            P(),
            P(),
            P(),
            P(),
        ),
        out_specs=P(("x", "z", "core", "head"), None),
        check_vma=False,
    )
```

```python
import jax
import jax.numpy as jnp
from jax import lax
from jax.sharding import PartitionSpec as P

ATTENTION_SPAN = 64
CH = 128


norm_eps = 0.00064
decay_floor = -0.5
highest = lax.Precision.HIGHEST


def shifted(value, axis, by):
    size = lax.axis_size(axis)
    pairs = [(i, i + by) for i in range(size) if 0 <= i + by < size]
    return lax.ppermute(value, axis, pairs)


def earlier_segment(prompt_label, position):
    earlier = lax.dynamic_slice_in_dim(prompt_label, jnp.maximum(position - 1, 0), 1, 0)
    return jnp.where(position > 0, earlier, jnp.full_like(earlier, -1))


def local(
    acceptance_linear,
    lookup_linear,
    payload_linear,
    valve_linear,
    layer_entries,
    prompt_label,
    fading_baseline,
    previous_mixing_share,
    fading_lower_map,
    fading_raise_map,
    diagonal_reward,
    cluster_gain_vector,
    cluster_mean_shift_add,
):
    head_count = lax.axis_size("head")
    seq_index = lax.axis_index(("x", "z", "core"))
    head_index = lax.axis_index("head")
    row_count = layer_entries.shape[0]
    block_start = (seq_index * head_count + head_index) * row_count
    own_seg = lax.dynamic_slice_in_dim(prompt_label, block_start, row_count, 0)
    prior_seg = jnp.concatenate([earlier_segment(prompt_label, block_start), own_seg[:-1]])
    edge_row = shifted(layer_entries[-1:], ("x", "z", "core", "head"), 1)
    prev_rows = jnp.concatenate([edge_row, layer_entries[:-1]], axis=0)
    prev_rows = jnp.where((prior_seg == own_seg)[:, None], prev_rows, jnp.zeros_like(prev_rows))
    current = layer_entries.astype(jnp.float32)
    blended_input = (
        current + (prev_rows.astype(jnp.float32) - current) * previous_mixing_share
    ).astype(jnp.bfloat16)
    decay_hidden_rows = jnp.tanh(
        jnp.dot(blended_input, fading_lower_map, preferred_element_type=jnp.float32)
    ).astype(jnp.bfloat16)
    decay_score = fading_baseline + jnp.dot(
        decay_hidden_rows, fading_raise_map, preferred_element_type=jnp.float32
    )
    log_decay = jnp.maximum(-jnp.exp(decay_score), decay_floor).astype(jnp.bfloat16)
    query_head, key_head, value_head, decay_head = (
        lax.all_to_all(acceptance_linear, "head", split_axis=1, concat_axis=0, tiled=True),
        lax.all_to_all(lookup_linear, "head", split_axis=1, concat_axis=0, tiled=True),
        lax.all_to_all(payload_linear, "head", split_axis=1, concat_axis=0, tiled=True),
        lax.all_to_all(log_decay, "head", split_axis=1, concat_axis=0, tiled=True),
    )
    tokens = query_head.shape[0]
    partition_extent = query_head.shape[1]
    local_heads = partition_extent // ATTENTION_SPAN
    stretches = tokens // CH
    seq_start = seq_index * tokens
    seg_block = lax.dynamic_slice_in_dim(prompt_label, seq_start, tokens, 0).reshape(stretches, CH)
    seg_before = earlier_segment(prompt_label, seq_start)
    stretch_prior = jnp.concatenate([seg_before, seg_block[:-1, -1]])
    feature_start = head_index * partition_extent
    partition_reward = lax.dynamic_slice_in_dim(
        diagonal_reward, feature_start, partition_extent, 0
    ).reshape(local_heads, ATTENTION_SPAN)
    gain_local = lax.dynamic_slice_in_dim(
        cluster_gain_vector, feature_start, partition_extent, 0
    ).reshape(local_heads, ATTENTION_SPAN)
    bias_local = lax.dynamic_slice_in_dim(
        cluster_mean_shift_add, feature_start, partition_extent, 0
    ).reshape(local_heads, ATTENTION_SPAN)
    blocked = (stretches, CH, local_heads, ATTENTION_SPAN)
    request_vectors = query_head.reshape(blocked).astype(jnp.float32)
    lookup_vectors = key_head.reshape(blocked).astype(jnp.float32)
    payload_vectors = value_head.reshape(blocked).astype(jnp.float32)
    decays = decay_head.reshape(blocked).astype(jnp.float32)
    cumulative = jnp.cumsum(decays, axis=1)
    before = cumulative - decays
    ending = cumulative[:, -1]
    scaled_query = request_vectors * jnp.exp(before)
    scaled_key = lookup_vectors * jnp.exp(-cumulative)
    scores = jnp.einsum("cthd,cshd->chts", scaled_query, scaled_key, precision=highest)
    causal = lax.broadcasted_iota(jnp.int32, (CH, CH), 0) > lax.broadcasted_iota(
        jnp.int32, (CH, CH), 1
    )
    allowed = causal[None] & (seg_block[:, :, None] == seg_block[:, None, :])
    scores = jnp.where(allowed[:, None], scores, jnp.zeros_like(scores))
    within = jnp.einsum("chts,cshd->cthd", scores, payload_vectors, precision=highest)
    diagonal_contribution = (
        jnp.sum(request_vectors * partition_reward * lookup_vectors, axis=3, keepdims=True)
        * payload_vectors
    )
    keep_last = (seg_block == seg_block[:, -1:]).astype(jnp.float32)
    tail_keys = lookup_vectors * jnp.exp(ending[:, None] - cumulative) * keep_last[:, :, None, None]
    stretch_state = jnp.einsum("cthd,cthe->chde", tail_keys, payload_vectors, precision=highest)
    stretch_decay = (
        jnp.exp(ending) * (seg_block[:, -1] == stretch_prior).astype(jnp.float32)[:, None, None]
    )

    def advance(carry_state, pieces):
        factor, new_part = pieces
        return (factor[:, :, None] * carry_state + new_part, carry_state)

    zero_state = jnp.zeros((local_heads, ATTENTION_SPAN, ATTENTION_SPAN), jnp.float32)
    span_state, local_start = lax.scan(advance, zero_state, (stretch_decay, stretch_state))

    def multiply(product, factor):
        return (product * factor, product)

    span_decay, decay_before = lax.scan(
        multiply, jnp.ones((local_heads, ATTENTION_SPAN), jnp.float32), stretch_decay
    )

    def fold(gathered, position):
        count = gathered.shape[0]
        prefix_state = jnp.zeros_like(gathered[0, :, :ATTENTION_SPAN])
        prefix_decay = jnp.ones_like(gathered[0, :, ATTENTION_SPAN])
        total_state, total_decay = prefix_state, prefix_decay
        for k in range(count):
            part_decay = gathered[k, :, ATTENTION_SPAN]
            part_state = gathered[k, :, :ATTENTION_SPAN]
            take = k < position
            prefix_state = jnp.where(
                take, part_decay[:, :, None] * prefix_state + part_state, prefix_state
            )
            prefix_decay = jnp.where(take, part_decay * prefix_decay, prefix_decay)
            total_state = part_decay[:, :, None] * total_state + part_state
            total_decay = part_decay * total_decay
        return (
            jnp.concatenate([prefix_state, prefix_decay[:, None, :]], axis=1),
            jnp.concatenate([total_state, total_decay[:, None, :]], axis=1),
        )

    own = jnp.concatenate([span_state, span_decay[:, None, :]], axis=1)
    core_index = lax.axis_index("core")
    core_count = lax.axis_size("core")
    core_prefix, core_total = fold(lax.all_gather(own, "core"), core_index)
    share = local_heads // core_count
    core_share = lax.dynamic_slice_in_dim(core_total, core_index * share, share, 0)
    z_prefix, z_total = fold(lax.all_gather(core_share, "z"), lax.axis_index("z"))
    x_prefix, _ = fold(lax.all_gather(z_total, "x"), lax.axis_index("x"))
    pair_incoming = (
        z_prefix[:, ATTENTION_SPAN][:, :, None] * x_prefix[:, :ATTENTION_SPAN]
        + z_prefix[:, :ATTENTION_SPAN]
    )
    pair_incoming = lax.all_gather(pair_incoming, "core", tiled=True)
    incoming = (
        core_prefix[:, ATTENTION_SPAN][:, :, None] * pair_incoming
        + core_prefix[:, :ATTENTION_SPAN]
    )
    start_state = local_start + decay_before[:, :, :, None] * incoming[None]
    keep_first = (seg_block == stretch_prior[:, None]).astype(jnp.float32)
    carried = jnp.einsum(
        "cthd,chde->cthe",
        scaled_query * keep_first[:, :, None, None],
        start_state,
        precision=highest,
    )
    mixing = within + diagonal_contribution + carried
    center = mixing - jnp.mean(mixing, axis=3, keepdims=True)
    spread = jnp.mean(center * center, axis=3, keepdims=True)
    normed = center * lax.rsqrt(spread + norm_eps) * gain_local + bias_local
    normed = normed.astype(jnp.bfloat16).reshape(tokens, partition_extent)
    returned = lax.all_to_all(normed, "head", split_axis=0, concat_axis=1, tiled=True)
    return (returned.astype(jnp.float32) * jax.nn.silu(valve_linear.astype(jnp.float32))).astype(
        jnp.bfloat16
    )


def solution(mesh):
    seq_count, head_count = mesh.devices.shape
    core_count = 2
    z_count = min(8, seq_count // core_count)
    fine_mesh = jax.sharding.Mesh(
        mesh.devices.reshape(seq_count // (z_count * core_count), z_count, core_count, head_count),
        ("x", "z", "core", "head"),
    )
    return jax.shard_map(
        local,
        mesh=fine_mesh,
        in_specs=(
            P(("x", "z", "core", "head"), None),
            P(("x", "z", "core", "head"), None),
            P(("x", "z", "core", "head"), None),
            P(("x", "z", "core", "head"), None),
            P(("x", "z", "core", "head"), None),
            P(),
            P(),
            P(),
            P(),
            P(),
            P(),
            P(),
            P(),
        ),
        out_specs=P(("x", "z", "core", "head"), None),
        check_vma=False,
    )
```

```python
import jax
import jax.numpy as jnp
from jax import lax
from jax.sharding import PartitionSpec as P

ATTENTION_SPAN = 64
CH = 128


norm_eps = 0.00064
decay_floor = -0.5
highest = lax.Precision.HIGH


def shifted(value, axis, by):
    size = lax.axis_size(axis)
    pairs = [(i, i + by) for i in range(size) if 0 <= i + by < size]
    return lax.ppermute(value, axis, pairs)


def earlier_segment(prompt_label, position):
    earlier = lax.dynamic_slice_in_dim(prompt_label, jnp.maximum(position - 1, 0), 1, 0)
    return jnp.where(position > 0, earlier, jnp.full_like(earlier, -1))


def local(
    acceptance_linear,
    lookup_linear,
    payload_linear,
    valve_linear,
    layer_entries,
    prompt_label,
    fading_baseline,
    previous_mixing_share,
    fading_lower_map,
    fading_raise_map,
    diagonal_reward,
    cluster_gain_vector,
    cluster_mean_shift_add,
):
    head_count = lax.axis_size("head")
    seq_index = lax.axis_index(("x", "z", "core"))
    head_index = lax.axis_index("head")
    row_count = layer_entries.shape[0]
    block_start = (seq_index * head_count + head_index) * row_count
    own_seg = lax.dynamic_slice_in_dim(prompt_label, block_start, row_count, 0)
    prior_seg = jnp.concatenate([earlier_segment(prompt_label, block_start), own_seg[:-1]])
    edge_row = shifted(layer_entries[-1:], ("x", "z", "core", "head"), 1)
    prev_rows = jnp.concatenate([edge_row, layer_entries[:-1]], axis=0)
    prev_rows = jnp.where((prior_seg == own_seg)[:, None], prev_rows, jnp.zeros_like(prev_rows))
    current = layer_entries.astype(jnp.float32)
    blended_input = (
        current + (prev_rows.astype(jnp.float32) - current) * previous_mixing_share
    ).astype(jnp.bfloat16)
    decay_hidden_rows = jnp.tanh(
        jnp.dot(blended_input, fading_lower_map, preferred_element_type=jnp.float32)
    ).astype(jnp.bfloat16)
    decay_score = fading_baseline + jnp.dot(
        decay_hidden_rows, fading_raise_map, preferred_element_type=jnp.float32
    )
    log_decay = jnp.maximum(-jnp.exp(decay_score), decay_floor).astype(jnp.bfloat16)
    query_head, key_head, value_head, decay_head = (
        lax.all_to_all(acceptance_linear, "head", split_axis=1, concat_axis=0, tiled=True),
        lax.all_to_all(lookup_linear, "head", split_axis=1, concat_axis=0, tiled=True),
        lax.all_to_all(payload_linear, "head", split_axis=1, concat_axis=0, tiled=True),
        lax.all_to_all(log_decay, "head", split_axis=1, concat_axis=0, tiled=True),
    )
    tokens = query_head.shape[0]
    partition_extent = query_head.shape[1]
    local_heads = partition_extent // ATTENTION_SPAN
    stretches = tokens // CH
    seq_start = seq_index * tokens
    seg_block = lax.dynamic_slice_in_dim(prompt_label, seq_start, tokens, 0).reshape(stretches, CH)
    seg_before = earlier_segment(prompt_label, seq_start)
    stretch_prior = jnp.concatenate([seg_before, seg_block[:-1, -1]])
    feature_start = head_index * partition_extent
    partition_reward = lax.dynamic_slice_in_dim(
        diagonal_reward, feature_start, partition_extent, 0
    ).reshape(local_heads, ATTENTION_SPAN)
    gain_local = lax.dynamic_slice_in_dim(
        cluster_gain_vector, feature_start, partition_extent, 0
    ).reshape(local_heads, ATTENTION_SPAN)
    bias_local = lax.dynamic_slice_in_dim(
        cluster_mean_shift_add, feature_start, partition_extent, 0
    ).reshape(local_heads, ATTENTION_SPAN)
    blocked = (stretches, CH, local_heads, ATTENTION_SPAN)
    request_vectors = query_head.reshape(blocked).astype(jnp.float32)
    lookup_vectors = key_head.reshape(blocked).astype(jnp.float32)
    payload_vectors = value_head.reshape(blocked).astype(jnp.float32)
    decays = decay_head.reshape(blocked).astype(jnp.float32)
    cumulative = jnp.cumsum(decays, axis=1)
    before = cumulative - decays
    ending = cumulative[:, -1]
    scaled_query = request_vectors * jnp.exp(before)
    scaled_key = lookup_vectors * jnp.exp(-cumulative)
    scores = jnp.einsum("cthd,cshd->chts", scaled_query, scaled_key, precision=highest)
    causal = lax.broadcasted_iota(jnp.int32, (CH, CH), 0) > lax.broadcasted_iota(
        jnp.int32, (CH, CH), 1
    )
    allowed = causal[None] & (seg_block[:, :, None] == seg_block[:, None, :])
    scores = jnp.where(allowed[:, None], scores, jnp.zeros_like(scores))
    within = jnp.einsum("chts,cshd->cthd", scores, payload_vectors, precision=highest)
    diagonal_contribution = (
        jnp.sum(request_vectors * partition_reward * lookup_vectors, axis=3, keepdims=True)
        * payload_vectors
    )
    keep_last = (seg_block == seg_block[:, -1:]).astype(jnp.float32)
    tail_keys = lookup_vectors * jnp.exp(ending[:, None] - cumulative) * keep_last[:, :, None, None]
    stretch_state = jnp.einsum("cthd,cthe->chde", tail_keys, payload_vectors, precision=highest)
    stretch_decay = (
        jnp.exp(ending) * (seg_block[:, -1] == stretch_prior).astype(jnp.float32)[:, None, None]
    )

    zero_state = jnp.zeros((local_heads, ATTENTION_SPAN, ATTENTION_SPAN), jnp.float32)
    span_state = zero_state
    span_decay = jnp.ones((local_heads, ATTENTION_SPAN), jnp.float32)
    starts, decays_before = [], []
    for stretch in range(stretches):
        starts.append(span_state)
        decays_before.append(span_decay)
        span_state = stretch_decay[stretch][:, :, None] * span_state + stretch_state[stretch]
        span_decay = span_decay * stretch_decay[stretch]
    local_start = jnp.stack(starts)
    decay_before = jnp.stack(decays_before)

    def fold(gathered, position):
        count = gathered.shape[0]
        prefix_state = jnp.zeros_like(gathered[0, :, :ATTENTION_SPAN])
        prefix_decay = jnp.ones_like(gathered[0, :, ATTENTION_SPAN])
        total_state, total_decay = prefix_state, prefix_decay
        for k in range(count):
            part_decay = gathered[k, :, ATTENTION_SPAN]
            part_state = gathered[k, :, :ATTENTION_SPAN]
            take = k < position
            prefix_state = jnp.where(
                take, part_decay[:, :, None] * prefix_state + part_state, prefix_state
            )
            prefix_decay = jnp.where(take, part_decay * prefix_decay, prefix_decay)
            total_state = part_decay[:, :, None] * total_state + part_state
            total_decay = part_decay * total_decay
        return (
            jnp.concatenate([prefix_state, prefix_decay[:, None, :]], axis=1),
            jnp.concatenate([total_state, total_decay[:, None, :]], axis=1),
        )

    own = jnp.concatenate([span_state, span_decay[:, None, :]], axis=1)
    core_index = lax.axis_index("core")
    core_count = lax.axis_size("core")
    core_prefix, core_total = fold(lax.all_gather(own, "core"), core_index)
    share = local_heads // core_count
    core_share = lax.dynamic_slice_in_dim(core_total, core_index * share, share, 0)
    z_prefix, z_total = fold(lax.all_gather(core_share, "z"), lax.axis_index("z"))
    x_prefix, _ = fold(lax.all_gather(z_total, "x"), lax.axis_index("x"))
    pair_incoming = (
        z_prefix[:, ATTENTION_SPAN][:, :, None] * x_prefix[:, :ATTENTION_SPAN]
        + z_prefix[:, :ATTENTION_SPAN]
    )
    pair_incoming = lax.all_gather(pair_incoming, "core", tiled=True)
    incoming = (
        core_prefix[:, ATTENTION_SPAN][:, :, None] * pair_incoming
        + core_prefix[:, :ATTENTION_SPAN]
    )
    start_state = local_start + decay_before[:, :, :, None] * incoming[None]
    keep_first = (seg_block == stretch_prior[:, None]).astype(jnp.float32)
    carried = jnp.einsum(
        "cthd,chde->cthe",
        scaled_query * keep_first[:, :, None, None],
        start_state,
        precision=highest,
    )
    mixing = within + diagonal_contribution + carried
    center = mixing - jnp.mean(mixing, axis=3, keepdims=True)
    spread = jnp.mean(center * center, axis=3, keepdims=True)
    normed = center * lax.rsqrt(spread + norm_eps) * gain_local + bias_local
    normed = normed.astype(jnp.bfloat16).reshape(tokens, partition_extent)
    returned = lax.all_to_all(normed, "head", split_axis=0, concat_axis=1, tiled=True)
    return (returned.astype(jnp.float32) * jax.nn.silu(valve_linear.astype(jnp.float32))).astype(
        jnp.bfloat16
    )


def solution(mesh):
    seq_count, head_count = mesh.devices.shape
    core_count = 2
    z_count = min(8, seq_count // core_count)
    fine_mesh = jax.sharding.Mesh(
        mesh.devices.reshape(seq_count // (z_count * core_count), z_count, core_count, head_count),
        ("x", "z", "core", "head"),
    )
    return jax.shard_map(
        local,
        mesh=fine_mesh,
        in_specs=(
            P(("x", "z", "core", "head"), None),
            P(("x", "z", "core", "head"), None),
            P(("x", "z", "core", "head"), None),
            P(("x", "z", "core", "head"), None),
            P(("x", "z", "core", "head"), None),
            P(),
            P(),
            P(),
            P(),
            P(),
            P(),
            P(),
            P(),
        ),
        out_specs=P(("x", "z", "core", "head"), None),
        check_vma=False,
    )
```

```python
import jax
import jax.numpy as jnp
from jax import lax
from jax.sharding import PartitionSpec as P

ATTENTION_SPAN = 64
CH = 128


norm_eps = 0.00064
decay_floor = -0.5
highest = lax.Precision.HIGH


def shifted(value, axis, by):
    size = lax.axis_size(axis)
    pairs = [(i, i + by) for i in range(size) if 0 <= i + by < size]
    return lax.ppermute(value, axis, pairs)


def earlier_segment(prompt_label, position):
    earlier = lax.dynamic_slice_in_dim(prompt_label, jnp.maximum(position - 1, 0), 1, 0)
    return jnp.where(position > 0, earlier, jnp.full_like(earlier, -1))


def local(
    acceptance_linear,
    lookup_linear,
    payload_linear,
    valve_linear,
    layer_entries,
    prompt_label,
    fading_baseline,
    previous_mixing_share,
    fading_lower_map,
    fading_raise_map,
    diagonal_reward,
    cluster_gain_vector,
    cluster_mean_shift_add,
):
    head_count = lax.axis_size("head")
    seq_index = lax.axis_index(("x", "zh", "zl", "core"))
    head_index = lax.axis_index("head")
    row_count = layer_entries.shape[0]
    block_start = (seq_index * head_count + head_index) * row_count
    own_seg = lax.dynamic_slice_in_dim(prompt_label, block_start, row_count, 0)
    prior_seg = jnp.concatenate([earlier_segment(prompt_label, block_start), own_seg[:-1]])
    edge_row = shifted(layer_entries[-1:], ("x", "zh", "zl", "core", "head"), 1)
    prev_rows = jnp.concatenate([edge_row, layer_entries[:-1]], axis=0)
    prev_rows = jnp.where((prior_seg == own_seg)[:, None], prev_rows, jnp.zeros_like(prev_rows))
    current = layer_entries.astype(jnp.float32)
    blended_input = (
        current + (prev_rows.astype(jnp.float32) - current) * previous_mixing_share
    ).astype(jnp.bfloat16)
    decay_hidden_rows = jnp.tanh(
        jnp.dot(blended_input, fading_lower_map, preferred_element_type=jnp.float32)
    ).astype(jnp.bfloat16)
    decay_score = fading_baseline + jnp.dot(
        decay_hidden_rows, fading_raise_map, preferred_element_type=jnp.float32
    )
    log_decay = jnp.maximum(-jnp.exp(decay_score), decay_floor).astype(jnp.bfloat16)
    query_head, key_head, value_head, decay_head = (
        lax.all_to_all(acceptance_linear, "head", split_axis=1, concat_axis=0, tiled=True),
        lax.all_to_all(lookup_linear, "head", split_axis=1, concat_axis=0, tiled=True),
        lax.all_to_all(payload_linear, "head", split_axis=1, concat_axis=0, tiled=True),
        lax.all_to_all(log_decay, "head", split_axis=1, concat_axis=0, tiled=True),
    )
    tokens = query_head.shape[0]
    partition_extent = query_head.shape[1]
    local_heads = partition_extent // ATTENTION_SPAN
    stretches = tokens // CH
    seq_start = seq_index * tokens
    seg_block = lax.dynamic_slice_in_dim(prompt_label, seq_start, tokens, 0).reshape(stretches, CH)
    seg_before = earlier_segment(prompt_label, seq_start)
    stretch_prior = jnp.concatenate([seg_before, seg_block[:-1, -1]])
    feature_start = head_index * partition_extent
    partition_reward = lax.dynamic_slice_in_dim(
        diagonal_reward, feature_start, partition_extent, 0
    ).reshape(local_heads, ATTENTION_SPAN)
    gain_local = lax.dynamic_slice_in_dim(
        cluster_gain_vector, feature_start, partition_extent, 0
    ).reshape(local_heads, ATTENTION_SPAN)
    bias_local = lax.dynamic_slice_in_dim(
        cluster_mean_shift_add, feature_start, partition_extent, 0
    ).reshape(local_heads, ATTENTION_SPAN)
    blocked = (stretches, CH, local_heads, ATTENTION_SPAN)
    request_vectors = query_head.reshape(blocked).astype(jnp.float32)
    lookup_vectors = key_head.reshape(blocked).astype(jnp.float32)
    payload_vectors = value_head.reshape(blocked).astype(jnp.float32)
    decays = decay_head.reshape(blocked).astype(jnp.float32)
    cumulative = jnp.cumsum(decays, axis=1)
    before = cumulative - decays
    ending = cumulative[:, -1]
    scaled_query = request_vectors * jnp.exp(before)
    scaled_key = lookup_vectors * jnp.exp(-cumulative)
    scores = jnp.einsum("cthd,cshd->chts", scaled_query, scaled_key, precision=highest)
    causal = lax.broadcasted_iota(jnp.int32, (CH, CH), 0) > lax.broadcasted_iota(
        jnp.int32, (CH, CH), 1
    )
    allowed = causal[None] & (seg_block[:, :, None] == seg_block[:, None, :])
    scores = jnp.where(allowed[:, None], scores, jnp.zeros_like(scores))
    within = jnp.einsum("chts,cshd->cthd", scores, payload_vectors, precision=highest)
    diagonal_contribution = (
        jnp.sum(request_vectors * partition_reward * lookup_vectors, axis=3, keepdims=True)
        * payload_vectors
    )
    keep_last = (seg_block == seg_block[:, -1:]).astype(jnp.float32)
    tail_keys = lookup_vectors * jnp.exp(ending[:, None] - cumulative) * keep_last[:, :, None, None]
    stretch_state = jnp.einsum("cthd,cthe->chde", tail_keys, payload_vectors, precision=highest)
    stretch_decay = (
        jnp.exp(ending) * (seg_block[:, -1] == stretch_prior).astype(jnp.float32)[:, None, None]
    )

    zero_state = jnp.zeros((local_heads, ATTENTION_SPAN, ATTENTION_SPAN), jnp.float32)
    span_state = zero_state
    span_decay = jnp.ones((local_heads, ATTENTION_SPAN), jnp.float32)
    starts, decays_before = [], []
    for stretch in range(stretches):
        starts.append(span_state)
        decays_before.append(span_decay)
        span_state = stretch_decay[stretch][:, :, None] * span_state + stretch_state[stretch]
        span_decay = span_decay * stretch_decay[stretch]
    local_start = jnp.stack(starts)
    decay_before = jnp.stack(decays_before)

    def fold(gathered, position):
        count = gathered.shape[0]
        prefix_state = jnp.zeros_like(gathered[0, :, :ATTENTION_SPAN])
        prefix_decay = jnp.ones_like(gathered[0, :, ATTENTION_SPAN])
        total_state, total_decay = prefix_state, prefix_decay
        for k in range(count):
            part_decay = gathered[k, :, ATTENTION_SPAN]
            part_state = gathered[k, :, :ATTENTION_SPAN]
            take = k < position
            prefix_state = jnp.where(
                take, part_decay[:, :, None] * prefix_state + part_state, prefix_state
            )
            prefix_decay = jnp.where(take, part_decay * prefix_decay, prefix_decay)
            total_state = part_decay[:, :, None] * total_state + part_state
            total_decay = part_decay * total_decay
        return (
            jnp.concatenate([prefix_state, prefix_decay[:, None, :]], axis=1),
            jnp.concatenate([total_state, total_decay[:, None, :]], axis=1),
        )

    own = jnp.concatenate([span_state, span_decay[:, None, :]], axis=1)
    core_index = lax.axis_index("core")
    core_count = lax.axis_size("core")
    core_prefix, core_total = fold(lax.all_gather(own, "core"), core_index)
    share = local_heads // core_count
    level_prefixes = []
    running = lax.dynamic_slice_in_dim(core_total, core_index * share, share, 0)
    for axis in ("zl", "zh", "x"):
        prefix, running = fold(lax.all_gather(running, axis), lax.axis_index(axis))
        level_prefixes.append(prefix)
    pair_incoming = level_prefixes[-1][:, :ATTENTION_SPAN]
    for prefix in level_prefixes[-2::-1]:
        pair_incoming = (
            prefix[:, ATTENTION_SPAN][:, :, None] * pair_incoming + prefix[:, :ATTENTION_SPAN]
        )
    pair_incoming = lax.all_gather(pair_incoming, "core", tiled=True)
    incoming = (
        core_prefix[:, ATTENTION_SPAN][:, :, None] * pair_incoming
        + core_prefix[:, :ATTENTION_SPAN]
    )
    start_state = local_start + decay_before[:, :, :, None] * incoming[None]
    keep_first = (seg_block == stretch_prior[:, None]).astype(jnp.float32)
    carried = jnp.einsum(
        "cthd,chde->cthe",
        scaled_query * keep_first[:, :, None, None],
        start_state,
        precision=highest,
    )
    mixing = within + diagonal_contribution + carried
    center = mixing - jnp.mean(mixing, axis=3, keepdims=True)
    spread = jnp.mean(center * center, axis=3, keepdims=True)
    normed = center * lax.rsqrt(spread + norm_eps) * gain_local + bias_local
    normed = normed.astype(jnp.bfloat16).reshape(tokens, partition_extent)
    returned = lax.all_to_all(normed, "head", split_axis=0, concat_axis=1, tiled=True)
    return (returned.astype(jnp.float32) * jax.nn.silu(valve_linear.astype(jnp.float32))).astype(
        jnp.bfloat16
    )


def solution(mesh):
    seq_count, head_count = mesh.devices.shape
    core_count = 2
    z_count = min(8, seq_count // core_count)
    z_low = min(4, z_count)
    fine_mesh = jax.sharding.Mesh(
        mesh.devices.reshape(
            seq_count // (z_count * core_count), z_count // z_low, z_low, core_count, head_count
        ),
        ("x", "zh", "zl", "core", "head"),
    )
    return jax.shard_map(
        local,
        mesh=fine_mesh,
        in_specs=(
            P(("x", "zh", "zl", "core", "head"), None),
            P(("x", "zh", "zl", "core", "head"), None),
            P(("x", "zh", "zl", "core", "head"), None),
            P(("x", "zh", "zl", "core", "head"), None),
            P(("x", "zh", "zl", "core", "head"), None),
            P(),
            P(),
            P(),
            P(),
            P(),
            P(),
            P(),
            P(),
        ),
        out_specs=P(("x", "zh", "zl", "core", "head"), None),
        check_vma=False,
    )
```

```python
import jax
import jax.numpy as jnp
from jax import lax
from jax.sharding import PartitionSpec as P

ATTENTION_SPAN = 64
CH = 128


norm_eps = 0.00064
decay_floor = -0.5
highest = lax.Precision.HIGH


def shifted(value, axis, by):
    size = lax.axis_size(axis)
    pairs = [(i, i + by) for i in range(size) if 0 <= i + by < size]
    return lax.ppermute(value, axis, pairs)


def earlier_segment(prompt_label, position):
    earlier = lax.dynamic_slice_in_dim(prompt_label, jnp.maximum(position - 1, 0), 1, 0)
    return jnp.where(position > 0, earlier, jnp.full_like(earlier, -1))


def local(
    acceptance_linear,
    lookup_linear,
    payload_linear,
    valve_linear,
    layer_entries,
    prompt_label,
    fading_baseline,
    previous_mixing_share,
    fading_lower_map,
    fading_raise_map,
    diagonal_reward,
    cluster_gain_vector,
    cluster_mean_shift_add,
):
    head_count = lax.axis_size("head")
    seq_index = lax.axis_index(("x", "zh", "zl", "core"))
    head_index = lax.axis_index("head")
    row_count = layer_entries.shape[0]
    block_start = (seq_index * head_count + head_index) * row_count
    own_seg = lax.dynamic_slice_in_dim(prompt_label, block_start, row_count, 0)
    prior_seg = jnp.concatenate([earlier_segment(prompt_label, block_start), own_seg[:-1]])
    edge_row = shifted(layer_entries[-1:], ("x", "zh", "zl", "core", "head"), 1)
    prev_rows = jnp.concatenate([edge_row, layer_entries[:-1]], axis=0)
    prev_rows = jnp.where((prior_seg == own_seg)[:, None], prev_rows, jnp.zeros_like(prev_rows))
    current = layer_entries.astype(jnp.float32)
    blended_input = (
        current + (prev_rows.astype(jnp.float32) - current) * previous_mixing_share
    ).astype(jnp.bfloat16)
    decay_hidden_rows = jnp.tanh(
        jnp.dot(blended_input, fading_lower_map, preferred_element_type=jnp.float32)
    ).astype(jnp.bfloat16)
    decay_score = fading_baseline + jnp.dot(
        decay_hidden_rows, fading_raise_map, preferred_element_type=jnp.float32
    )
    log_decay = jnp.maximum(-jnp.exp(decay_score), decay_floor).astype(jnp.bfloat16)
    moved = lax.all_to_all(
        jnp.stack([acceptance_linear, lookup_linear, payload_linear, log_decay]),
        "head",
        split_axis=2,
        concat_axis=1,
        tiled=True,
    )
    query_head, key_head, value_head, decay_head = moved[0], moved[1], moved[2], moved[3]
    tokens = query_head.shape[0]
    partition_extent = query_head.shape[1]
    local_heads = partition_extent // ATTENTION_SPAN
    stretches = tokens // CH
    seq_start = seq_index * tokens
    seg_block = lax.dynamic_slice_in_dim(prompt_label, seq_start, tokens, 0).reshape(stretches, CH)
    seg_before = earlier_segment(prompt_label, seq_start)
    stretch_prior = jnp.concatenate([seg_before, seg_block[:-1, -1]])
    feature_start = head_index * partition_extent
    partition_reward = lax.dynamic_slice_in_dim(
        diagonal_reward, feature_start, partition_extent, 0
    ).reshape(local_heads, ATTENTION_SPAN)
    gain_local = lax.dynamic_slice_in_dim(
        cluster_gain_vector, feature_start, partition_extent, 0
    ).reshape(local_heads, ATTENTION_SPAN)
    bias_local = lax.dynamic_slice_in_dim(
        cluster_mean_shift_add, feature_start, partition_extent, 0
    ).reshape(local_heads, ATTENTION_SPAN)
    blocked = (stretches, CH, local_heads, ATTENTION_SPAN)
    request_vectors = query_head.reshape(blocked).astype(jnp.float32)
    lookup_vectors = key_head.reshape(blocked).astype(jnp.float32)
    payload_vectors = value_head.reshape(blocked).astype(jnp.float32)
    decays = decay_head.reshape(blocked).astype(jnp.float32)
    cumulative = jnp.cumsum(decays, axis=1)
    before = cumulative - decays
    ending = cumulative[:, -1]
    scaled_query = request_vectors * jnp.exp(before)
    scaled_key = lookup_vectors * jnp.exp(-cumulative)
    scores = jnp.einsum("cthd,cshd->chts", scaled_query, scaled_key, precision=highest)
    causal = lax.broadcasted_iota(jnp.int32, (CH, CH), 0) > lax.broadcasted_iota(
        jnp.int32, (CH, CH), 1
    )
    allowed = causal[None] & (seg_block[:, :, None] == seg_block[:, None, :])
    scores = jnp.where(allowed[:, None], scores, jnp.zeros_like(scores))
    within = jnp.einsum("chts,cshd->cthd", scores, payload_vectors, precision=highest)
    diagonal_contribution = (
        jnp.sum(request_vectors * partition_reward * lookup_vectors, axis=3, keepdims=True)
        * payload_vectors
    )
    keep_last = (seg_block == seg_block[:, -1:]).astype(jnp.float32)
    tail_keys = lookup_vectors * jnp.exp(ending[:, None] - cumulative) * keep_last[:, :, None, None]
    stretch_state = jnp.einsum("cthd,cthe->chde", tail_keys, payload_vectors, precision=highest)
    stretch_decay = (
        jnp.exp(ending) * (seg_block[:, -1] == stretch_prior).astype(jnp.float32)[:, None, None]
    )

    zero_state = jnp.zeros((local_heads, ATTENTION_SPAN, ATTENTION_SPAN), jnp.float32)
    span_state = zero_state
    span_decay = jnp.ones((local_heads, ATTENTION_SPAN), jnp.float32)
    starts, decays_before = [], []
    for stretch in range(stretches):
        starts.append(span_state)
        decays_before.append(span_decay)
        span_state = stretch_decay[stretch][:, :, None] * span_state + stretch_state[stretch]
        span_decay = span_decay * stretch_decay[stretch]
    local_start = jnp.stack(starts)
    decay_before = jnp.stack(decays_before)

    def fold(gathered, position):
        count = gathered.shape[0]
        prefix_state = jnp.zeros_like(gathered[0, :, :ATTENTION_SPAN])
        prefix_decay = jnp.ones_like(gathered[0, :, ATTENTION_SPAN])
        total_state, total_decay = prefix_state, prefix_decay
        for k in range(count):
            part_decay = gathered[k, :, ATTENTION_SPAN]
            part_state = gathered[k, :, :ATTENTION_SPAN]
            take = k < position
            prefix_state = jnp.where(
                take, part_decay[:, :, None] * prefix_state + part_state, prefix_state
            )
            prefix_decay = jnp.where(take, part_decay * prefix_decay, prefix_decay)
            total_state = part_decay[:, :, None] * total_state + part_state
            total_decay = part_decay * total_decay
        return (
            jnp.concatenate([prefix_state, prefix_decay[:, None, :]], axis=1),
            jnp.concatenate([total_state, total_decay[:, None, :]], axis=1),
        )

    own = jnp.concatenate([span_state, span_decay[:, None, :]], axis=1)
    core_index = lax.axis_index("core")
    core_count = lax.axis_size("core")
    core_prefix, core_total = fold(lax.all_gather(own, "core"), core_index)
    share = local_heads // core_count
    level_prefixes = []
    running = lax.dynamic_slice_in_dim(core_total, core_index * share, share, 0)
    for axis in ("zl", "zh", "x"):
        prefix, running = fold(lax.all_gather(running, axis), lax.axis_index(axis))
        level_prefixes.append(prefix)
    pair_incoming = level_prefixes[-1][:, :ATTENTION_SPAN]
    for prefix in level_prefixes[-2::-1]:
        pair_incoming = (
            prefix[:, ATTENTION_SPAN][:, :, None] * pair_incoming + prefix[:, :ATTENTION_SPAN]
        )
    pair_incoming = lax.all_gather(pair_incoming, "core", tiled=True)
    incoming = (
        core_prefix[:, ATTENTION_SPAN][:, :, None] * pair_incoming
        + core_prefix[:, :ATTENTION_SPAN]
    )
    start_state = local_start + decay_before[:, :, :, None] * incoming[None]
    keep_first = (seg_block == stretch_prior[:, None]).astype(jnp.float32)
    carried = jnp.einsum(
        "cthd,chde->cthe",
        scaled_query * keep_first[:, :, None, None],
        start_state,
        precision=highest,
    )
    mixing = within + diagonal_contribution + carried
    center = mixing - jnp.mean(mixing, axis=3, keepdims=True)
    spread = jnp.mean(center * center, axis=3, keepdims=True)
    normed = center * lax.rsqrt(spread + norm_eps) * gain_local + bias_local
    normed = normed.astype(jnp.bfloat16).reshape(tokens, partition_extent)
    returned = lax.all_to_all(normed, "head", split_axis=0, concat_axis=1, tiled=True)
    return (returned.astype(jnp.float32) * jax.nn.silu(valve_linear.astype(jnp.float32))).astype(
        jnp.bfloat16
    )


def solution(mesh):
    seq_count, head_count = mesh.devices.shape
    core_count = 2
    z_count = min(8, seq_count // core_count)
    z_low = min(4, z_count)
    fine_mesh = jax.sharding.Mesh(
        mesh.devices.reshape(
            seq_count // (z_count * core_count), z_count // z_low, z_low, core_count, head_count
        ),
        ("x", "zh", "zl", "core", "head"),
    )
    return jax.shard_map(
        local,
        mesh=fine_mesh,
        in_specs=(
            P(("x", "zh", "zl", "core", "head"), None),
            P(("x", "zh", "zl", "core", "head"), None),
            P(("x", "zh", "zl", "core", "head"), None),
            P(("x", "zh", "zl", "core", "head"), None),
            P(("x", "zh", "zl", "core", "head"), None),
            P(),
            P(),
            P(),
            P(),
            P(),
            P(),
            P(),
            P(),
        ),
        out_specs=P(("x", "zh", "zl", "core", "head"), None),
        check_vma=False,
    )
```

```python
import jax
import jax.numpy as jnp
from jax import lax
from jax.sharding import PartitionSpec as P

ATTENTION_SPAN = 64
CH = 128


norm_eps = 0.00064
decay_floor = -0.5
highest = lax.Precision.HIGH


def shifted(value, axis, by):
    size = lax.axis_size(axis)
    pairs = [(i, i + by) for i in range(size) if 0 <= i + by < size]
    return lax.ppermute(value, axis, pairs)


def earlier_segment(prompt_label, position):
    earlier = lax.dynamic_slice_in_dim(prompt_label, jnp.maximum(position - 1, 0), 1, 0)
    return jnp.where(position > 0, earlier, jnp.full_like(earlier, -1))


def local(
    acceptance_linear,
    lookup_linear,
    payload_linear,
    valve_linear,
    layer_entries,
    prompt_label,
    fading_baseline,
    previous_mixing_share,
    fading_lower_map,
    fading_raise_map,
    diagonal_reward,
    cluster_gain_vector,
    cluster_mean_shift_add,
):
    head_count = lax.axis_size("head")
    seq_index = lax.axis_index(("x", "zh", "zl", "core"))
    head_index = lax.axis_index("head")
    row_count = layer_entries.shape[0]
    block_start = (seq_index * head_count + head_index) * row_count
    own_seg = lax.dynamic_slice_in_dim(prompt_label, block_start, row_count, 0)
    prior_seg = jnp.concatenate([earlier_segment(prompt_label, block_start), own_seg[:-1]])
    edge_row = shifted(layer_entries[-1:], ("x", "zh", "zl", "core", "head"), 1)
    prev_rows = jnp.concatenate([edge_row, layer_entries[:-1]], axis=0)
    prev_rows = jnp.where((prior_seg == own_seg)[:, None], prev_rows, jnp.zeros_like(prev_rows))
    current = layer_entries.astype(jnp.float32)
    blended_input = (
        current + (prev_rows.astype(jnp.float32) - current) * previous_mixing_share
    ).astype(jnp.bfloat16)
    decay_hidden_rows = jnp.tanh(
        jnp.dot(blended_input, fading_lower_map, preferred_element_type=jnp.float32)
    ).astype(jnp.bfloat16)
    decay_score = fading_baseline + jnp.dot(
        decay_hidden_rows, fading_raise_map, preferred_element_type=jnp.float32
    )
    log_decay = jnp.maximum(-jnp.exp(decay_score), decay_floor).astype(jnp.bfloat16)
    assert row_count == CH
    total_heads = layer_entries.shape[1] // ATTENTION_SPAN
    local_heads = total_heads // head_count
    per_head = (row_count, total_heads, ATTENTION_SPAN)
    request_vectors = acceptance_linear.reshape(per_head).astype(jnp.float32)
    lookup_vectors = lookup_linear.reshape(per_head).astype(jnp.float32)
    payload_vectors = payload_linear.reshape(per_head).astype(jnp.float32)
    decays = log_decay.reshape(per_head).astype(jnp.float32)
    chunk_prior = earlier_segment(prompt_label, block_start)
    reward = diagonal_reward.reshape(total_heads, ATTENTION_SPAN)
    gain = cluster_gain_vector.reshape(total_heads, ATTENTION_SPAN)
    bias = cluster_mean_shift_add.reshape(total_heads, ATTENTION_SPAN)
    cumulative = jnp.cumsum(decays, axis=0)
    before = cumulative - decays
    ending = cumulative[-1]
    scaled_query = request_vectors * jnp.exp(before)
    scaled_key = lookup_vectors * jnp.exp(-cumulative)
    keep_last = (own_seg == own_seg[-1]).astype(jnp.float32)
    tail_keys = lookup_vectors * jnp.exp(ending[None] - cumulative) * keep_last[:, None, None]
    chunk_state = jnp.einsum("thd,the->hde", tail_keys, payload_vectors, precision=highest)
    chunk_decay = jnp.exp(ending) * (own_seg[-1] == chunk_prior).astype(jnp.float32)
    summary = jnp.concatenate([chunk_state, chunk_decay[:, None, :]], axis=1)
    summary = summary.reshape(head_count, local_heads, ATTENTION_SPAN + 1, ATTENTION_SPAN)
    summary = lax.all_to_all(summary, "head", split_axis=0, concat_axis=0, tiled=True)
    stretch_state = summary[:, :, :ATTENTION_SPAN]
    stretch_decay = summary[:, :, ATTENTION_SPAN]
    stretches = head_count

    zero_state = jnp.zeros((local_heads, ATTENTION_SPAN, ATTENTION_SPAN), jnp.float32)
    span_state = zero_state
    span_decay = jnp.ones((local_heads, ATTENTION_SPAN), jnp.float32)
    starts, decays_before = [], []
    for stretch in range(stretches):
        starts.append(span_state)
        decays_before.append(span_decay)
        span_state = stretch_decay[stretch][:, :, None] * span_state + stretch_state[stretch]
        span_decay = span_decay * stretch_decay[stretch]
    local_start = jnp.stack(starts)
    decay_before = jnp.stack(decays_before)

    def fold(gathered, position):
        count = gathered.shape[0]
        prefix_state = jnp.zeros_like(gathered[0, :, :ATTENTION_SPAN])
        prefix_decay = jnp.ones_like(gathered[0, :, ATTENTION_SPAN])
        total_state, total_decay = prefix_state, prefix_decay
        for k in range(count):
            part_decay = gathered[k, :, ATTENTION_SPAN]
            part_state = gathered[k, :, :ATTENTION_SPAN]
            take = k < position
            prefix_state = jnp.where(
                take, part_decay[:, :, None] * prefix_state + part_state, prefix_state
            )
            prefix_decay = jnp.where(take, part_decay * prefix_decay, prefix_decay)
            total_state = part_decay[:, :, None] * total_state + part_state
            total_decay = part_decay * total_decay
        return (
            jnp.concatenate([prefix_state, prefix_decay[:, None, :]], axis=1),
            jnp.concatenate([total_state, total_decay[:, None, :]], axis=1),
        )

    own = jnp.concatenate([span_state, span_decay[:, None, :]], axis=1)
    core_index = lax.axis_index("core")
    core_count = lax.axis_size("core")
    core_prefix, core_total = fold(lax.all_gather(own, "core"), core_index)
    share = local_heads // core_count
    level_prefixes = []
    running = lax.dynamic_slice_in_dim(core_total, core_index * share, share, 0)
    for axis in ("zl", "zh", "x"):
        prefix, running = fold(lax.all_gather(running, axis), lax.axis_index(axis))
        level_prefixes.append(prefix)
    pair_incoming = level_prefixes[-1][:, :ATTENTION_SPAN]
    for prefix in level_prefixes[-2::-1]:
        pair_incoming = (
            prefix[:, ATTENTION_SPAN][:, :, None] * pair_incoming + prefix[:, :ATTENTION_SPAN]
        )
    pair_incoming = lax.all_gather(pair_incoming, "core", tiled=True)
    incoming = (
        core_prefix[:, ATTENTION_SPAN][:, :, None] * pair_incoming
        + core_prefix[:, :ATTENTION_SPAN]
    )
    start_state = local_start + decay_before[:, :, :, None] * incoming[None]
    start_state = lax.all_to_all(start_state, "head", split_axis=0, concat_axis=0, tiled=True)
    start_state = start_state.reshape(total_heads, ATTENTION_SPAN, ATTENTION_SPAN)

    scores = jnp.einsum("thd,shd->hts", scaled_query, scaled_key, precision=highest)
    causal = lax.broadcasted_iota(jnp.int32, (CH, CH), 0) > lax.broadcasted_iota(
        jnp.int32, (CH, CH), 1
    )
    allowed = causal & (own_seg[:, None] == own_seg[None, :])
    scores = jnp.where(allowed[None], scores, jnp.zeros_like(scores))
    within = jnp.einsum("hts,shd->thd", scores, payload_vectors, precision=highest)
    diagonal_contribution = (
        jnp.sum(request_vectors * reward * lookup_vectors, axis=2, keepdims=True)
        * payload_vectors
    )
    keep_first = (own_seg == chunk_prior).astype(jnp.float32)
    carried = jnp.einsum(
        "thd,hde->the",
        scaled_query * keep_first[:, None, None],
        start_state,
        precision=highest,
    )
    mixing = within + diagonal_contribution + carried
    center = mixing - jnp.mean(mixing, axis=2, keepdims=True)
    spread = jnp.mean(center * center, axis=2, keepdims=True)
    normed = center * lax.rsqrt(spread + norm_eps) * gain + bias
    normed = normed.astype(jnp.bfloat16).reshape(layer_entries.shape)
    return (normed.astype(jnp.float32) * jax.nn.silu(valve_linear.astype(jnp.float32))).astype(
        jnp.bfloat16
    )


def solution(mesh):
    seq_count, head_count = mesh.devices.shape
    core_count = 2
    z_count = min(8, seq_count // core_count)
    z_low = min(4, z_count)
    fine_mesh = jax.sharding.Mesh(
        mesh.devices.reshape(
            seq_count // (z_count * core_count), z_count // z_low, z_low, core_count, head_count
        ),
        ("x", "zh", "zl", "core", "head"),
    )
    return jax.shard_map(
        local,
        mesh=fine_mesh,
        in_specs=(
            P(("x", "zh", "zl", "core", "head"), None),
            P(("x", "zh", "zl", "core", "head"), None),
            P(("x", "zh", "zl", "core", "head"), None),
            P(("x", "zh", "zl", "core", "head"), None),
            P(("x", "zh", "zl", "core", "head"), None),
            P(),
            P(),
            P(),
            P(),
            P(),
            P(),
            P(),
            P(),
        ),
        out_specs=P(("x", "zh", "zl", "core", "head"), None),
        check_vma=False,
    )
```

```python
import jax
import jax.numpy as jnp
from jax import lax
from jax.sharding import PartitionSpec as P

ATTENTION_SPAN = 64
CH = 128


norm_eps = 0.00064
decay_floor = -0.5
highest = lax.Precision.HIGH


def shifted(value, axis, by):
    size = lax.axis_size(axis)
    pairs = [(i, i + by) for i in range(size) if 0 <= i + by < size]
    return lax.ppermute(value, axis, pairs)


def earlier_segment(prompt_label, position):
    earlier = lax.dynamic_slice_in_dim(prompt_label, jnp.maximum(position - 1, 0), 1, 0)
    return jnp.where(position > 0, earlier, jnp.full_like(earlier, -1))


def local(
    acceptance_linear,
    lookup_linear,
    payload_linear,
    valve_linear,
    layer_entries,
    prompt_label,
    fading_baseline,
    previous_mixing_share,
    fading_lower_map,
    fading_raise_map,
    diagonal_reward,
    cluster_gain_vector,
    cluster_mean_shift_add,
):
    head_count = lax.axis_size("head")
    seq_index = lax.axis_index(("x", "zh", "zl", "core"))
    head_index = lax.axis_index("head")
    row_count = layer_entries.shape[0]
    block_start = (seq_index * head_count + head_index) * row_count
    own_seg = lax.dynamic_slice_in_dim(prompt_label, block_start, row_count, 0)
    prior_seg = jnp.concatenate([earlier_segment(prompt_label, block_start), own_seg[:-1]])
    edge_row = shifted(layer_entries[-1:], ("x", "zh", "zl", "core", "head"), 1)
    prev_rows = jnp.concatenate([edge_row, layer_entries[:-1]], axis=0)
    prev_rows = jnp.where((prior_seg == own_seg)[:, None], prev_rows, jnp.zeros_like(prev_rows))
    current = layer_entries.astype(jnp.float32)
    blended_input = (
        current + (prev_rows.astype(jnp.float32) - current) * previous_mixing_share
    ).astype(jnp.bfloat16)
    decay_hidden_rows = jnp.tanh(
        jnp.dot(blended_input, fading_lower_map, preferred_element_type=jnp.float32)
    ).astype(jnp.bfloat16)
    decay_score = fading_baseline + jnp.dot(
        decay_hidden_rows, fading_raise_map, preferred_element_type=jnp.float32
    )
    log_decay = jnp.maximum(-jnp.exp(decay_score), decay_floor).astype(jnp.bfloat16)
    query_head, key_head, value_head, decay_head = (
        lax.all_to_all(acceptance_linear, "head", split_axis=1, concat_axis=0, tiled=True),
        lax.all_to_all(lookup_linear, "head", split_axis=1, concat_axis=0, tiled=True),
        lax.all_to_all(payload_linear, "head", split_axis=1, concat_axis=0, tiled=True),
        lax.all_to_all(log_decay, "head", split_axis=1, concat_axis=0, tiled=True),
    )
    tokens = query_head.shape[0]
    partition_extent = query_head.shape[1]
    local_heads = partition_extent // ATTENTION_SPAN
    stretches = tokens // CH
    seq_start = seq_index * tokens
    seg_block = lax.dynamic_slice_in_dim(prompt_label, seq_start, tokens, 0).reshape(stretches, CH)
    seg_before = earlier_segment(prompt_label, seq_start)
    stretch_prior = jnp.concatenate([seg_before, seg_block[:-1, -1]])
    feature_start = head_index * partition_extent
    partition_reward = lax.dynamic_slice_in_dim(
        diagonal_reward, feature_start, partition_extent, 0
    ).reshape(local_heads, ATTENTION_SPAN)
    gain_local = lax.dynamic_slice_in_dim(
        cluster_gain_vector, feature_start, partition_extent, 0
    ).reshape(local_heads, ATTENTION_SPAN)
    bias_local = lax.dynamic_slice_in_dim(
        cluster_mean_shift_add, feature_start, partition_extent, 0
    ).reshape(local_heads, ATTENTION_SPAN)
    blocked = (stretches, CH, local_heads, ATTENTION_SPAN)
    request_vectors = query_head.reshape(blocked).astype(jnp.float32)
    lookup_vectors = key_head.reshape(blocked).astype(jnp.float32)
    payload_vectors = value_head.reshape(blocked).astype(jnp.float32)
    decays = decay_head.reshape(blocked).astype(jnp.float32)
    cumulative = jnp.cumsum(decays, axis=1)
    before = cumulative - decays
    ending = cumulative[:, -1]
    scaled_query = request_vectors * jnp.exp(before)
    scaled_key = lookup_vectors * jnp.exp(-cumulative)
    scores = jnp.einsum("cthd,cshd->chts", scaled_query, scaled_key, precision=highest)
    causal = lax.broadcasted_iota(jnp.int32, (CH, CH), 0) > lax.broadcasted_iota(
        jnp.int32, (CH, CH), 1
    )
    allowed = causal[None] & (seg_block[:, :, None] == seg_block[:, None, :])
    scores = jnp.where(allowed[:, None], scores, jnp.zeros_like(scores))
    within = jnp.einsum("chts,cshd->cthd", scores, payload_vectors, precision=highest)
    diagonal_contribution = (
        jnp.sum(request_vectors * partition_reward * lookup_vectors, axis=3, keepdims=True)
        * payload_vectors
    )
    keep_last = (seg_block == seg_block[:, -1:]).astype(jnp.float32)
    tail_keys = lookup_vectors * jnp.exp(ending[:, None] - cumulative) * keep_last[:, :, None, None]
    stretch_state = jnp.einsum("cthd,cthe->chde", tail_keys, payload_vectors, precision=highest)
    stretch_decay = (
        jnp.exp(ending) * (seg_block[:, -1] == stretch_prior).astype(jnp.float32)[:, None, None]
    )

    zero_state = jnp.zeros((local_heads, ATTENTION_SPAN, ATTENTION_SPAN), jnp.float32)
    span_state = zero_state
    span_decay = jnp.ones((local_heads, ATTENTION_SPAN), jnp.float32)
    starts, decays_before = [], []
    for stretch in range(stretches):
        starts.append(span_state)
        decays_before.append(span_decay)
        span_state = stretch_decay[stretch][:, :, None] * span_state + stretch_state[stretch]
        span_decay = span_decay * stretch_decay[stretch]
    local_start = jnp.stack(starts)
    decay_before = jnp.stack(decays_before)

    def fold(gathered, position):
        count = gathered.shape[0]
        prefix_state = jnp.zeros_like(gathered[0, :, :ATTENTION_SPAN])
        prefix_decay = jnp.ones_like(gathered[0, :, ATTENTION_SPAN])
        total_state, total_decay = prefix_state, prefix_decay
        for k in range(count):
            part_decay = gathered[k, :, ATTENTION_SPAN]
            part_state = gathered[k, :, :ATTENTION_SPAN]
            take = k < position
            prefix_state = jnp.where(
                take, part_decay[:, :, None] * prefix_state + part_state, prefix_state
            )
            prefix_decay = jnp.where(take, part_decay * prefix_decay, prefix_decay)
            total_state = part_decay[:, :, None] * total_state + part_state
            total_decay = part_decay * total_decay
        return (
            jnp.concatenate([prefix_state, prefix_decay[:, None, :]], axis=1),
            jnp.concatenate([total_state, total_decay[:, None, :]], axis=1),
        )

    own = jnp.concatenate([span_state, span_decay[:, None, :]], axis=1)
    core_index = lax.axis_index("core")
    core_count = lax.axis_size("core")
    core_prefix, core_total = fold(lax.all_gather(own, "core"), core_index)
    share = local_heads // core_count
    level_prefixes = []
    running = lax.dynamic_slice_in_dim(core_total, core_index * share, share, 0)
    for axis in ("zl", "zh", "x"):
        prefix, running = fold(lax.all_gather(running, axis), lax.axis_index(axis))
        level_prefixes.append(prefix)
    pair_incoming = level_prefixes[-1][:, :ATTENTION_SPAN]
    for prefix in level_prefixes[-2::-1]:
        pair_incoming = (
            prefix[:, ATTENTION_SPAN][:, :, None] * pair_incoming + prefix[:, :ATTENTION_SPAN]
        )
    pair_incoming = lax.all_gather(pair_incoming, "core", tiled=True)
    incoming = (
        core_prefix[:, ATTENTION_SPAN][:, :, None] * pair_incoming
        + core_prefix[:, :ATTENTION_SPAN]
    )
    start_state = local_start + decay_before[:, :, :, None] * incoming[None]
    keep_first = (seg_block == stretch_prior[:, None]).astype(jnp.float32)
    carried = jnp.einsum(
        "cthd,chde->cthe",
        scaled_query * keep_first[:, :, None, None],
        start_state,
        precision=highest,
    )
    mixing = within + diagonal_contribution + carried
    center = mixing - jnp.mean(mixing, axis=3, keepdims=True)
    spread = jnp.mean(center * center, axis=3, keepdims=True)
    normed = center * lax.rsqrt(spread + norm_eps) * gain_local + bias_local
    normed = normed.astype(jnp.bfloat16).reshape(tokens, partition_extent)
    returned = lax.all_to_all(normed, "head", split_axis=0, concat_axis=1, tiled=True)
    return (returned.astype(jnp.float32) * jax.nn.silu(valve_linear.astype(jnp.float32))).astype(
        jnp.bfloat16
    )


def solution(mesh):
    seq_count, head_count = mesh.devices.shape
    core_count = 2
    z_count = min(8, seq_count // core_count)
    z_low = min(2, z_count)
    fine_mesh = jax.sharding.Mesh(
        mesh.devices.reshape(
            seq_count // (z_count * core_count), z_count // z_low, z_low, core_count, head_count
        ),
        ("x", "zh", "zl", "core", "head"),
    )
    return jax.shard_map(
        local,
        mesh=fine_mesh,
        in_specs=(
            P(("x", "zh", "zl", "core", "head"), None),
            P(("x", "zh", "zl", "core", "head"), None),
            P(("x", "zh", "zl", "core", "head"), None),
            P(("x", "zh", "zl", "core", "head"), None),
            P(("x", "zh", "zl", "core", "head"), None),
            P(),
            P(),
            P(),
            P(),
            P(),
            P(),
            P(),
            P(),
        ),
        out_specs=P(("x", "zh", "zl", "core", "head"), None),
        check_vma=False,
    )
```

```python
import jax
import jax.numpy as jnp
from jax import lax
from jax.sharding import PartitionSpec as P

ATTENTION_SPAN = 64
CH = 128


norm_eps = 0.00064
decay_floor = -0.5
highest = lax.Precision.HIGH


def shifted(value, axis, by):
    size = lax.axis_size(axis)
    pairs = [(i, i + by) for i in range(size) if 0 <= i + by < size]
    return lax.ppermute(value, axis, pairs)


def earlier_segment(prompt_label, position):
    earlier = lax.dynamic_slice_in_dim(prompt_label, jnp.maximum(position - 1, 0), 1, 0)
    return jnp.where(position > 0, earlier, jnp.full_like(earlier, -1))


def local(
    acceptance_linear,
    lookup_linear,
    payload_linear,
    valve_linear,
    layer_entries,
    prompt_label,
    fading_baseline,
    previous_mixing_share,
    fading_lower_map,
    fading_raise_map,
    diagonal_reward,
    cluster_gain_vector,
    cluster_mean_shift_add,
):
    head_count = lax.axis_size("head")
    seq_index = lax.axis_index(("x", "zh", "zl", "core"))
    head_index = lax.axis_index("head")
    row_count = layer_entries.shape[0]
    block_start = (seq_index * head_count + head_index) * row_count
    own_seg = lax.dynamic_slice_in_dim(prompt_label, block_start, row_count, 0)
    prior_seg = jnp.concatenate([earlier_segment(prompt_label, block_start), own_seg[:-1]])
    edge_row = shifted(layer_entries[-1:], ("x", "zh", "zl", "core", "head"), 1)
    prev_rows = jnp.concatenate([edge_row, layer_entries[:-1]], axis=0)
    prev_rows = jnp.where((prior_seg == own_seg)[:, None], prev_rows, jnp.zeros_like(prev_rows))
    current = layer_entries.astype(jnp.float32)
    blended_input = (
        current + (prev_rows.astype(jnp.float32) - current) * previous_mixing_share
    ).astype(jnp.bfloat16)
    decay_hidden_rows = jnp.tanh(
        jnp.dot(blended_input, fading_lower_map, preferred_element_type=jnp.float32)
    ).astype(jnp.bfloat16)
    decay_score = fading_baseline + jnp.dot(
        decay_hidden_rows, fading_raise_map, preferred_element_type=jnp.float32
    )
    log_decay = jnp.maximum(-jnp.exp(decay_score), decay_floor).astype(jnp.bfloat16)
    query_head, key_head, value_head, decay_head = (
        lax.all_to_all(acceptance_linear, "head", split_axis=1, concat_axis=0, tiled=True),
        lax.all_to_all(lookup_linear, "head", split_axis=1, concat_axis=0, tiled=True),
        lax.all_to_all(payload_linear, "head", split_axis=1, concat_axis=0, tiled=True),
        lax.all_to_all(log_decay, "head", split_axis=1, concat_axis=0, tiled=True),
    )
    tokens = query_head.shape[0]
    partition_extent = query_head.shape[1]
    local_heads = partition_extent // ATTENTION_SPAN
    stretches = tokens // CH
    seq_start = seq_index * tokens
    seg_block = lax.dynamic_slice_in_dim(prompt_label, seq_start, tokens, 0).reshape(stretches, CH)
    seg_before = earlier_segment(prompt_label, seq_start)
    stretch_prior = jnp.concatenate([seg_before, seg_block[:-1, -1]])
    feature_start = head_index * partition_extent
    partition_reward = lax.dynamic_slice_in_dim(
        diagonal_reward, feature_start, partition_extent, 0
    ).reshape(local_heads, ATTENTION_SPAN)
    gain_local = lax.dynamic_slice_in_dim(
        cluster_gain_vector, feature_start, partition_extent, 0
    ).reshape(local_heads, ATTENTION_SPAN)
    bias_local = lax.dynamic_slice_in_dim(
        cluster_mean_shift_add, feature_start, partition_extent, 0
    ).reshape(local_heads, ATTENTION_SPAN)
    blocked = (stretches, CH, local_heads, ATTENTION_SPAN)
    request_vectors = query_head.reshape(blocked).astype(jnp.float32)
    lookup_vectors = key_head.reshape(blocked).astype(jnp.float32)
    payload_vectors = value_head.reshape(blocked).astype(jnp.float32)
    decays = decay_head.reshape(blocked).astype(jnp.float32)
    cumulative = jnp.cumsum(decays, axis=1)
    before = cumulative - decays
    ending = cumulative[:, -1]
    scaled_query = request_vectors * jnp.exp(before)
    scaled_key = lookup_vectors * jnp.exp(-cumulative)
    scores = jnp.einsum("cthd,cshd->chts", scaled_query, scaled_key, precision=highest)
    causal = lax.broadcasted_iota(jnp.int32, (CH, CH), 0) > lax.broadcasted_iota(
        jnp.int32, (CH, CH), 1
    )
    allowed = causal[None] & (seg_block[:, :, None] == seg_block[:, None, :])
    scores = jnp.where(allowed[:, None], scores, jnp.zeros_like(scores))
    within = jnp.einsum("chts,cshd->cthd", scores, payload_vectors, precision=highest)
    diagonal_contribution = (
        jnp.sum(request_vectors * partition_reward * lookup_vectors, axis=3, keepdims=True)
        * payload_vectors
    )
    keep_last = (seg_block == seg_block[:, -1:]).astype(jnp.float32)
    tail_keys = lookup_vectors * jnp.exp(ending[:, None] - cumulative) * keep_last[:, :, None, None]
    stretch_state = jnp.einsum("cthd,cthe->chde", tail_keys, payload_vectors, precision=highest)
    stretch_decay = (
        jnp.exp(ending) * (seg_block[:, -1] == stretch_prior).astype(jnp.float32)[:, None, None]
    )

    zero_state = jnp.zeros((local_heads, ATTENTION_SPAN, ATTENTION_SPAN), jnp.float32)
    span_state = zero_state
    span_decay = jnp.ones((local_heads, ATTENTION_SPAN), jnp.float32)
    starts, decays_before = [], []
    for stretch in range(stretches):
        starts.append(span_state)
        decays_before.append(span_decay)
        span_state = stretch_decay[stretch][:, :, None] * span_state + stretch_state[stretch]
        span_decay = span_decay * stretch_decay[stretch]
    local_start = jnp.stack(starts)
    decay_before = jnp.stack(decays_before)

    def fold(gathered, position):
        count = gathered.shape[0]
        prefix_state = jnp.zeros_like(gathered[0, :, :ATTENTION_SPAN])
        prefix_decay = jnp.ones_like(gathered[0, :, ATTENTION_SPAN])
        total_state, total_decay = prefix_state, prefix_decay
        for k in range(count):
            part_decay = gathered[k, :, ATTENTION_SPAN]
            part_state = gathered[k, :, :ATTENTION_SPAN]
            take = k < position
            prefix_state = jnp.where(
                take, part_decay[:, :, None] * prefix_state + part_state, prefix_state
            )
            prefix_decay = jnp.where(take, part_decay * prefix_decay, prefix_decay)
            total_state = part_decay[:, :, None] * total_state + part_state
            total_decay = part_decay * total_decay
        return (
            jnp.concatenate([prefix_state, prefix_decay[:, None, :]], axis=1),
            jnp.concatenate([total_state, total_decay[:, None, :]], axis=1),
        )

    own = jnp.concatenate([span_state, span_decay[:, None, :]], axis=1)
    core_index = lax.axis_index("core")
    core_count = lax.axis_size("core")
    core_prefix, core_total = fold(lax.all_gather(own, "core"), core_index)
    share = local_heads // core_count
    level_prefixes = []
    running = lax.dynamic_slice_in_dim(core_total, core_index * share, share, 0)
    for axis in ("zl", "zh", "x"):
        position = lax.axis_index(axis)
        if lax.axis_size(axis) == 2:
            partner = lax.ppermute(running, axis, [(0, 1), (1, 0)])
            gathered = jnp.where(
                position == 0, jnp.stack([running, partner]), jnp.stack([partner, running])
            )
        else:
            gathered = lax.all_gather(running, axis)
        prefix, running = fold(gathered, position)
        level_prefixes.append(prefix)
    pair_incoming = level_prefixes[-1][:, :ATTENTION_SPAN]
    for prefix in level_prefixes[-2::-1]:
        pair_incoming = (
            prefix[:, ATTENTION_SPAN][:, :, None] * pair_incoming + prefix[:, :ATTENTION_SPAN]
        )
    pair_incoming = lax.all_gather(pair_incoming, "core", tiled=True)
    incoming = (
        core_prefix[:, ATTENTION_SPAN][:, :, None] * pair_incoming
        + core_prefix[:, :ATTENTION_SPAN]
    )
    start_state = local_start + decay_before[:, :, :, None] * incoming[None]
    keep_first = (seg_block == stretch_prior[:, None]).astype(jnp.float32)
    carried = jnp.einsum(
        "cthd,chde->cthe",
        scaled_query * keep_first[:, :, None, None],
        start_state,
        precision=highest,
    )
    mixing = within + diagonal_contribution + carried
    center = mixing - jnp.mean(mixing, axis=3, keepdims=True)
    spread = jnp.mean(center * center, axis=3, keepdims=True)
    normed = center * lax.rsqrt(spread + norm_eps) * gain_local + bias_local
    normed = normed.astype(jnp.bfloat16).reshape(tokens, partition_extent)
    returned = lax.all_to_all(normed, "head", split_axis=0, concat_axis=1, tiled=True)
    return (returned.astype(jnp.float32) * jax.nn.silu(valve_linear.astype(jnp.float32))).astype(
        jnp.bfloat16
    )


def solution(mesh):
    seq_count, head_count = mesh.devices.shape
    core_count = 2
    z_count = min(8, seq_count // core_count)
    z_low = min(2, z_count)
    fine_mesh = jax.sharding.Mesh(
        mesh.devices.reshape(
            seq_count // (z_count * core_count), z_count // z_low, z_low, core_count, head_count
        ),
        ("x", "zh", "zl", "core", "head"),
    )
    return jax.shard_map(
        local,
        mesh=fine_mesh,
        in_specs=(
            P(("x", "zh", "zl", "core", "head"), None),
            P(("x", "zh", "zl", "core", "head"), None),
            P(("x", "zh", "zl", "core", "head"), None),
            P(("x", "zh", "zl", "core", "head"), None),
            P(("x", "zh", "zl", "core", "head"), None),
            P(),
            P(),
            P(),
            P(),
            P(),
            P(),
            P(),
            P(),
        ),
        out_specs=P(("x", "zh", "zl", "core", "head"), None),
        check_vma=False,
    )
```

```python
import jax
import jax.numpy as jnp
from jax import lax
from jax.sharding import PartitionSpec as P

ATTENTION_SPAN = 64
CH = 128


norm_eps = 0.00064
decay_floor = -0.5
highest = lax.Precision.HIGH


def shifted(value, axis, by):
    size = lax.axis_size(axis)
    pairs = [(i, i + by) for i in range(size) if 0 <= i + by < size]
    return lax.ppermute(value, axis, pairs)


def earlier_segment(prompt_label, position):
    earlier = lax.dynamic_slice_in_dim(prompt_label, jnp.maximum(position - 1, 0), 1, 0)
    return jnp.where(position > 0, earlier, jnp.full_like(earlier, -1))


def local(
    acceptance_linear,
    lookup_linear,
    payload_linear,
    valve_linear,
    layer_entries,
    prompt_label,
    fading_baseline,
    previous_mixing_share,
    fading_lower_map,
    fading_raise_map,
    diagonal_reward,
    cluster_gain_vector,
    cluster_mean_shift_add,
):
    head_count = lax.axis_size("head")
    seq_index = lax.axis_index(("x", "zh", "zl", "core"))
    head_index = lax.axis_index("head")
    row_count = layer_entries.shape[0]
    block_start = (seq_index * head_count + head_index) * row_count
    own_seg = lax.dynamic_slice_in_dim(prompt_label, block_start, row_count, 0)
    prior_seg = jnp.concatenate([earlier_segment(prompt_label, block_start), own_seg[:-1]])
    edge_row = shifted(layer_entries[-1:], ("x", "zh", "zl", "core", "head"), 1)
    prev_rows = jnp.concatenate([edge_row, layer_entries[:-1]], axis=0)
    prev_rows = jnp.where((prior_seg == own_seg)[:, None], prev_rows, jnp.zeros_like(prev_rows))
    current = layer_entries.astype(jnp.float32)
    blended_input = (
        current + (prev_rows.astype(jnp.float32) - current) * previous_mixing_share
    ).astype(jnp.bfloat16)
    decay_hidden_rows = jnp.tanh(
        jnp.dot(blended_input, fading_lower_map, preferred_element_type=jnp.float32)
    ).astype(jnp.bfloat16)
    decay_score = fading_baseline + jnp.dot(
        decay_hidden_rows, fading_raise_map, preferred_element_type=jnp.float32
    )
    log_decay = jnp.maximum(-jnp.exp(decay_score), decay_floor).astype(jnp.bfloat16)
    query_head, key_head, value_head, decay_head = (
        lax.all_to_all(acceptance_linear, "head", split_axis=1, concat_axis=0, tiled=True),
        lax.all_to_all(lookup_linear, "head", split_axis=1, concat_axis=0, tiled=True),
        lax.all_to_all(payload_linear, "head", split_axis=1, concat_axis=0, tiled=True),
        lax.all_to_all(log_decay, "head", split_axis=1, concat_axis=0, tiled=True),
    )
    tokens = query_head.shape[0]
    partition_extent = query_head.shape[1]
    local_heads = partition_extent // ATTENTION_SPAN
    stretches = tokens // CH
    seq_start = seq_index * tokens
    seg_block = lax.dynamic_slice_in_dim(prompt_label, seq_start, tokens, 0).reshape(stretches, CH)
    seg_before = earlier_segment(prompt_label, seq_start)
    stretch_prior = jnp.concatenate([seg_before, seg_block[:-1, -1]])
    feature_start = head_index * partition_extent
    partition_reward = lax.dynamic_slice_in_dim(
        diagonal_reward, feature_start, partition_extent, 0
    ).reshape(local_heads, ATTENTION_SPAN)
    gain_local = lax.dynamic_slice_in_dim(
        cluster_gain_vector, feature_start, partition_extent, 0
    ).reshape(local_heads, ATTENTION_SPAN)
    bias_local = lax.dynamic_slice_in_dim(
        cluster_mean_shift_add, feature_start, partition_extent, 0
    ).reshape(local_heads, ATTENTION_SPAN)
    blocked = (stretches, CH, local_heads, ATTENTION_SPAN)
    request_vectors = query_head.reshape(blocked).astype(jnp.float32)
    lookup_vectors = key_head.reshape(blocked).astype(jnp.float32)
    payload_vectors = value_head.reshape(blocked).astype(jnp.float32)
    decays = decay_head.reshape(blocked).astype(jnp.float32)
    cumulative = jnp.cumsum(decays, axis=1)
    before = cumulative - decays
    ending = cumulative[:, -1]
    scaled_query = request_vectors * jnp.exp(before)
    scaled_key = lookup_vectors * jnp.exp(-cumulative)
    scores = jnp.einsum("cthd,cshd->chts", scaled_query, scaled_key, precision=highest)
    causal = lax.broadcasted_iota(jnp.int32, (CH, CH), 0) > lax.broadcasted_iota(
        jnp.int32, (CH, CH), 1
    )
    allowed = causal[None] & (seg_block[:, :, None] == seg_block[:, None, :])
    scores = jnp.where(allowed[:, None], scores, jnp.zeros_like(scores))
    within = jnp.einsum("chts,cshd->cthd", scores, payload_vectors, precision=highest)
    diagonal_contribution = (
        jnp.sum(request_vectors * partition_reward * lookup_vectors, axis=3, keepdims=True)
        * payload_vectors
    )
    keep_last = (seg_block == seg_block[:, -1:]).astype(jnp.float32)
    tail_keys = lookup_vectors * jnp.exp(ending[:, None] - cumulative) * keep_last[:, :, None, None]
    stretch_state = jnp.einsum("cthd,cthe->chde", tail_keys, payload_vectors, precision=highest)
    stretch_decay = (
        jnp.exp(ending) * (seg_block[:, -1] == stretch_prior).astype(jnp.float32)[:, None, None]
    )

    zero_state = jnp.zeros((local_heads, ATTENTION_SPAN, ATTENTION_SPAN), jnp.float32)
    span_state = zero_state
    span_decay = jnp.ones((local_heads, ATTENTION_SPAN), jnp.float32)
    starts, decays_before = [], []
    for stretch in range(stretches):
        starts.append(span_state)
        decays_before.append(span_decay)
        span_state = stretch_decay[stretch][:, :, None] * span_state + stretch_state[stretch]
        span_decay = span_decay * stretch_decay[stretch]
    local_start = jnp.stack(starts)
    decay_before = jnp.stack(decays_before)

    def fold(gathered, position):
        count = gathered.shape[0]
        prefix_state = jnp.zeros_like(gathered[0, :, :ATTENTION_SPAN])
        prefix_decay = jnp.ones_like(gathered[0, :, ATTENTION_SPAN])
        total_state, total_decay = prefix_state, prefix_decay
        for k in range(count):
            part_decay = gathered[k, :, ATTENTION_SPAN]
            part_state = gathered[k, :, :ATTENTION_SPAN]
            take = k < position
            prefix_state = jnp.where(
                take, part_decay[:, :, None] * prefix_state + part_state, prefix_state
            )
            prefix_decay = jnp.where(take, part_decay * prefix_decay, prefix_decay)
            total_state = part_decay[:, :, None] * total_state + part_state
            total_decay = part_decay * total_decay
        return (
            jnp.concatenate([prefix_state, prefix_decay[:, None, :]], axis=1),
            jnp.concatenate([total_state, total_decay[:, None, :]], axis=1),
        )

    own = jnp.concatenate([span_state, span_decay[:, None, :]], axis=1)
    core_index = lax.axis_index("core")
    core_count = lax.axis_size("core")
    core_prefix, core_total = fold(lax.all_gather(own, "core"), core_index)
    share = local_heads // core_count
    level_prefixes = []
    running = lax.dynamic_slice_in_dim(core_total, core_index * share, share, 0)
    for axis in ("zl", "zh", "x"):
        position = lax.axis_index(axis)
        count = lax.axis_size(axis)
        gathered = running[None]
        distance = 1
        while distance < count:
            partner = lax.ppermute(
                gathered, axis, [(i, i ^ distance) for i in range(count)]
            )
            gathered = jnp.where(
                (position // distance) % 2 == 0,
                jnp.concatenate([gathered, partner]),
                jnp.concatenate([partner, gathered]),
            )
            distance *= 2
        prefix, running = fold(gathered, position)
        level_prefixes.append(prefix)
    pair_incoming = level_prefixes[-1][:, :ATTENTION_SPAN]
    for prefix in level_prefixes[-2::-1]:
        pair_incoming = (
            prefix[:, ATTENTION_SPAN][:, :, None] * pair_incoming + prefix[:, :ATTENTION_SPAN]
        )
    pair_incoming = lax.all_gather(pair_incoming, "core", tiled=True)
    incoming = (
        core_prefix[:, ATTENTION_SPAN][:, :, None] * pair_incoming
        + core_prefix[:, :ATTENTION_SPAN]
    )
    start_state = local_start + decay_before[:, :, :, None] * incoming[None]
    keep_first = (seg_block == stretch_prior[:, None]).astype(jnp.float32)
    carried = jnp.einsum(
        "cthd,chde->cthe",
        scaled_query * keep_first[:, :, None, None],
        start_state,
        precision=highest,
    )
    mixing = within + diagonal_contribution + carried
    center = mixing - jnp.mean(mixing, axis=3, keepdims=True)
    spread = jnp.mean(center * center, axis=3, keepdims=True)
    normed = center * lax.rsqrt(spread + norm_eps) * gain_local + bias_local
    normed = normed.astype(jnp.bfloat16).reshape(tokens, partition_extent)
    returned = lax.all_to_all(normed, "head", split_axis=0, concat_axis=1, tiled=True)
    return (returned.astype(jnp.float32) * jax.nn.silu(valve_linear.astype(jnp.float32))).astype(
        jnp.bfloat16
    )


def solution(mesh):
    seq_count, head_count = mesh.devices.shape
    core_count = 2
    z_count = min(8, seq_count // core_count)
    z_low = min(2, z_count)
    fine_mesh = jax.sharding.Mesh(
        mesh.devices.reshape(
            seq_count // (z_count * core_count), z_count // z_low, z_low, core_count, head_count
        ),
        ("x", "zh", "zl", "core", "head"),
    )
    return jax.shard_map(
        local,
        mesh=fine_mesh,
        in_specs=(
            P(("x", "zh", "zl", "core", "head"), None),
            P(("x", "zh", "zl", "core", "head"), None),
            P(("x", "zh", "zl", "core", "head"), None),
            P(("x", "zh", "zl", "core", "head"), None),
            P(("x", "zh", "zl", "core", "head"), None),
            P(),
            P(),
            P(),
            P(),
            P(),
            P(),
            P(),
            P(),
        ),
        out_specs=P(("x", "zh", "zl", "core", "head"), None),
        check_vma=False,
    )
```

```python
import jax
import jax.numpy as jnp
from jax import lax
from jax.sharding import PartitionSpec as P

ATTENTION_SPAN = 64
CH = 128


norm_eps = 0.00064
decay_floor = -0.5
highest = lax.Precision.HIGH


def shifted(value, axis, by):
    size = lax.axis_size(axis)
    pairs = [(i, i + by) for i in range(size) if 0 <= i + by < size]
    return lax.ppermute(value, axis, pairs)


def earlier_segment(prompt_label, position):
    earlier = lax.dynamic_slice_in_dim(prompt_label, jnp.maximum(position - 1, 0), 1, 0)
    return jnp.where(position > 0, earlier, jnp.full_like(earlier, -1))


def local(
    acceptance_linear,
    lookup_linear,
    payload_linear,
    valve_linear,
    layer_entries,
    prompt_label,
    fading_baseline,
    previous_mixing_share,
    fading_lower_map,
    fading_raise_map,
    diagonal_reward,
    cluster_gain_vector,
    cluster_mean_shift_add,
):
    head_count = lax.axis_size("head")
    seq_index = lax.axis_index(("x", "zh", "zl", "core"))
    head_index = lax.axis_index("head")
    row_count = layer_entries.shape[0]
    block_start = (seq_index * head_count + head_index) * row_count
    own_seg = lax.dynamic_slice_in_dim(prompt_label, block_start, row_count, 0)
    prior_seg = jnp.concatenate([earlier_segment(prompt_label, block_start), own_seg[:-1]])
    edge_row = shifted(layer_entries[-1:], ("x", "zh", "zl", "core", "head"), 1)
    prev_rows = jnp.concatenate([edge_row, layer_entries[:-1]], axis=0)
    prev_rows = jnp.where((prior_seg == own_seg)[:, None], prev_rows, jnp.zeros_like(prev_rows))
    current = layer_entries.astype(jnp.float32)
    blended_input = (
        current + (prev_rows.astype(jnp.float32) - current) * previous_mixing_share
    ).astype(jnp.bfloat16)
    decay_hidden_rows = jnp.tanh(
        jnp.dot(blended_input, fading_lower_map, preferred_element_type=jnp.float32)
    ).astype(jnp.bfloat16)
    decay_score = fading_baseline + jnp.dot(
        decay_hidden_rows, fading_raise_map, preferred_element_type=jnp.float32
    )
    log_decay = jnp.maximum(-jnp.exp(decay_score), decay_floor).astype(jnp.bfloat16)
    query_head, key_head, value_head, decay_head = (
        lax.all_to_all(acceptance_linear, "head", split_axis=1, concat_axis=0, tiled=True),
        lax.all_to_all(lookup_linear, "head", split_axis=1, concat_axis=0, tiled=True),
        lax.all_to_all(payload_linear, "head", split_axis=1, concat_axis=0, tiled=True),
        lax.all_to_all(log_decay, "head", split_axis=1, concat_axis=0, tiled=True),
    )
    tokens = query_head.shape[0]
    partition_extent = query_head.shape[1]
    local_heads = partition_extent // ATTENTION_SPAN
    stretches = tokens // CH
    seq_start = seq_index * tokens
    seg_block = lax.dynamic_slice_in_dim(prompt_label, seq_start, tokens, 0).reshape(stretches, CH)
    seg_before = earlier_segment(prompt_label, seq_start)
    stretch_prior = jnp.concatenate([seg_before, seg_block[:-1, -1]])
    feature_start = head_index * partition_extent
    partition_reward = lax.dynamic_slice_in_dim(
        diagonal_reward, feature_start, partition_extent, 0
    ).reshape(local_heads, ATTENTION_SPAN)
    gain_local = lax.dynamic_slice_in_dim(
        cluster_gain_vector, feature_start, partition_extent, 0
    ).reshape(local_heads, ATTENTION_SPAN)
    bias_local = lax.dynamic_slice_in_dim(
        cluster_mean_shift_add, feature_start, partition_extent, 0
    ).reshape(local_heads, ATTENTION_SPAN)
    blocked = (stretches, CH, local_heads, ATTENTION_SPAN)
    request_vectors = query_head.reshape(blocked).astype(jnp.float32)
    lookup_vectors = key_head.reshape(blocked).astype(jnp.float32)
    payload_vectors = value_head.reshape(blocked).astype(jnp.float32)
    decays = decay_head.reshape(blocked).astype(jnp.float32)
    cumulative = jnp.cumsum(decays, axis=1)
    before = cumulative - decays
    ending = cumulative[:, -1]
    scaled_query = request_vectors * jnp.exp(before)
    scaled_key = lookup_vectors * jnp.exp(-cumulative)
    scores = jnp.einsum("cthd,cshd->chts", scaled_query, scaled_key, precision=highest)
    causal = lax.broadcasted_iota(jnp.int32, (CH, CH), 0) > lax.broadcasted_iota(
        jnp.int32, (CH, CH), 1
    )
    allowed = causal[None] & (seg_block[:, :, None] == seg_block[:, None, :])
    scores = jnp.where(allowed[:, None], scores, jnp.zeros_like(scores))
    within = jnp.einsum("chts,cshd->cthd", scores, payload_vectors, precision=highest)
    diagonal_contribution = (
        jnp.sum(request_vectors * partition_reward * lookup_vectors, axis=3, keepdims=True)
        * payload_vectors
    )
    keep_last = (seg_block == seg_block[:, -1:]).astype(jnp.float32)
    tail_keys = lookup_vectors * jnp.exp(ending[:, None] - cumulative) * keep_last[:, :, None, None]
    stretch_state = jnp.einsum("cthd,cthe->chde", tail_keys, payload_vectors, precision=highest)
    stretch_decay = (
        jnp.exp(ending) * (seg_block[:, -1] == stretch_prior).astype(jnp.float32)[:, None, None]
    )

    zero_state = jnp.zeros((local_heads, ATTENTION_SPAN, ATTENTION_SPAN), jnp.float32)
    span_state = zero_state
    span_decay = jnp.ones((local_heads, ATTENTION_SPAN), jnp.float32)
    starts, decays_before = [], []
    for stretch in range(stretches):
        starts.append(span_state)
        decays_before.append(span_decay)
        span_state = stretch_decay[stretch][:, :, None] * span_state + stretch_state[stretch]
        span_decay = span_decay * stretch_decay[stretch]
    local_start = jnp.stack(starts)
    decay_before = jnp.stack(decays_before)

    def fold(gathered, position):
        count = gathered.shape[0]
        prefix_state = jnp.zeros_like(gathered[0, :, :ATTENTION_SPAN])
        prefix_decay = jnp.ones_like(gathered[0, :, ATTENTION_SPAN])
        total_state, total_decay = prefix_state, prefix_decay
        for k in range(count):
            part_decay = gathered[k, :, ATTENTION_SPAN]
            part_state = gathered[k, :, :ATTENTION_SPAN]
            take = k < position
            prefix_state = jnp.where(
                take, part_decay[:, :, None] * prefix_state + part_state, prefix_state
            )
            prefix_decay = jnp.where(take, part_decay * prefix_decay, prefix_decay)
            total_state = part_decay[:, :, None] * total_state + part_state
            total_decay = part_decay * total_decay
        return (
            jnp.concatenate([prefix_state, prefix_decay[:, None, :]], axis=1),
            jnp.concatenate([total_state, total_decay[:, None, :]], axis=1),
        )

    own = jnp.concatenate([span_state, span_decay[:, None, :]], axis=1)
    core_index = lax.axis_index("core")
    core_count = lax.axis_size("core")
    core_prefix, core_total = fold(lax.all_gather(own, "core"), core_index)
    share = local_heads // core_count
    level_prefixes = []
    running = lax.dynamic_slice_in_dim(core_total, core_index * share, share, 0)
    for axis in ("zl", "zh", "x"):
        position = lax.axis_index(axis)
        if lax.axis_size(axis) == 2:
            partner = lax.ppermute(running, axis, [(0, 1), (1, 0)])
            gathered = jnp.where(
                position == 0, jnp.stack([running, partner]), jnp.stack([partner, running])
            )
        else:
            gathered = lax.all_gather(running, axis)
        prefix, running = fold(gathered, position)
        level_prefixes.append(prefix)
    pair_incoming = level_prefixes[-1][:, :ATTENTION_SPAN]
    for prefix in level_prefixes[-2::-1]:
        pair_incoming = (
            prefix[:, ATTENTION_SPAN][:, :, None] * pair_incoming + prefix[:, :ATTENTION_SPAN]
        )
    pair_incoming = lax.all_gather(pair_incoming, "core", tiled=True)
    incoming = (
        core_prefix[:, ATTENTION_SPAN][:, :, None] * pair_incoming
        + core_prefix[:, :ATTENTION_SPAN]
    )
    start_state = local_start + decay_before[:, :, :, None] * incoming[None]
    keep_first = (seg_block == stretch_prior[:, None]).astype(jnp.float32)
    carried = jnp.einsum(
        "cthd,chde->cthe",
        scaled_query * keep_first[:, :, None, None],
        start_state,
        precision=highest,
    )
    local_part = lax.optimization_barrier(within + diagonal_contribution)
    mixing = local_part + carried
    center = mixing - jnp.mean(mixing, axis=3, keepdims=True)
    spread = jnp.mean(center * center, axis=3, keepdims=True)
    normed = center * lax.rsqrt(spread + norm_eps) * gain_local + bias_local
    normed = normed.astype(jnp.bfloat16).reshape(tokens, partition_extent)
    returned = lax.all_to_all(normed, "head", split_axis=0, concat_axis=1, tiled=True)
    return (returned.astype(jnp.float32) * jax.nn.silu(valve_linear.astype(jnp.float32))).astype(
        jnp.bfloat16
    )


def solution(mesh):
    seq_count, head_count = mesh.devices.shape
    core_count = 2
    z_count = min(8, seq_count // core_count)
    z_low = min(2, z_count)
    fine_mesh = jax.sharding.Mesh(
        mesh.devices.reshape(
            seq_count // (z_count * core_count), z_count // z_low, z_low, core_count, head_count
        ),
        ("x", "zh", "zl", "core", "head"),
    )
    return jax.shard_map(
        local,
        mesh=fine_mesh,
        in_specs=(
            P(("x", "zh", "zl", "core", "head"), None),
            P(("x", "zh", "zl", "core", "head"), None),
            P(("x", "zh", "zl", "core", "head"), None),
            P(("x", "zh", "zl", "core", "head"), None),
            P(("x", "zh", "zl", "core", "head"), None),
            P(),
            P(),
            P(),
            P(),
            P(),
            P(),
            P(),
            P(),
        ),
        out_specs=P(("x", "zh", "zl", "core", "head"), None),
        check_vma=False,
    )
```

```python
import jax
import jax.numpy as jnp
from jax import lax
from jax.sharding import PartitionSpec as P

ATTENTION_SPAN = 64
CH = 128


norm_eps = 0.00064
decay_floor = -0.5
highest = lax.Precision.HIGH


def shifted(value, axis, by):
    size = lax.axis_size(axis)
    pairs = [(i, i + by) for i in range(size) if 0 <= i + by < size]
    return lax.ppermute(value, axis, pairs)


def earlier_segment(prompt_label, position):
    earlier = lax.dynamic_slice_in_dim(prompt_label, jnp.maximum(position - 1, 0), 1, 0)
    return jnp.where(position > 0, earlier, jnp.full_like(earlier, -1))


def local(
    acceptance_linear,
    lookup_linear,
    payload_linear,
    valve_linear,
    layer_entries,
    prompt_label,
    fading_baseline,
    previous_mixing_share,
    fading_lower_map,
    fading_raise_map,
    diagonal_reward,
    cluster_gain_vector,
    cluster_mean_shift_add,
):
    head_count = lax.axis_size("head")
    seq_index = lax.axis_index(("x", "zh", "zl", "core"))
    head_index = lax.axis_index("head")
    row_count = layer_entries.shape[0]
    block_start = (seq_index * head_count + head_index) * row_count
    own_seg = lax.dynamic_slice_in_dim(prompt_label, block_start, row_count, 0)
    prior_seg = jnp.concatenate([earlier_segment(prompt_label, block_start), own_seg[:-1]])
    edge_row = shifted(layer_entries[-1:], ("x", "zh", "zl", "core", "head"), 1)
    prev_rows = jnp.concatenate([edge_row, layer_entries[:-1]], axis=0)
    prev_rows = jnp.where((prior_seg == own_seg)[:, None], prev_rows, jnp.zeros_like(prev_rows))
    current = layer_entries.astype(jnp.float32)
    blended_input = (
        current + (prev_rows.astype(jnp.float32) - current) * previous_mixing_share
    ).astype(jnp.bfloat16)
    decay_hidden_rows = jnp.tanh(
        jnp.dot(blended_input, fading_lower_map, preferred_element_type=jnp.float32)
    ).astype(jnp.bfloat16)
    decay_score = fading_baseline + jnp.dot(
        decay_hidden_rows, fading_raise_map, preferred_element_type=jnp.float32
    )
    log_decay = jnp.maximum(-jnp.exp(decay_score), decay_floor).astype(jnp.bfloat16)
    query_head, key_head, value_head, decay_head = (
        lax.all_to_all(acceptance_linear, "head", split_axis=1, concat_axis=0, tiled=True),
        lax.all_to_all(lookup_linear, "head", split_axis=1, concat_axis=0, tiled=True),
        lax.all_to_all(payload_linear, "head", split_axis=1, concat_axis=0, tiled=True),
        lax.all_to_all(log_decay, "head", split_axis=1, concat_axis=0, tiled=True),
    )
    tokens = query_head.shape[0]
    partition_extent = query_head.shape[1]
    local_heads = partition_extent // ATTENTION_SPAN
    stretches = tokens // CH
    seq_start = seq_index * tokens
    seg_block = lax.dynamic_slice_in_dim(prompt_label, seq_start, tokens, 0).reshape(stretches, CH)
    seg_before = earlier_segment(prompt_label, seq_start)
    stretch_prior = jnp.concatenate([seg_before, seg_block[:-1, -1]])
    feature_start = head_index * partition_extent
    partition_reward = lax.dynamic_slice_in_dim(
        diagonal_reward, feature_start, partition_extent, 0
    ).reshape(local_heads, ATTENTION_SPAN)
    gain_local = lax.dynamic_slice_in_dim(
        cluster_gain_vector, feature_start, partition_extent, 0
    ).reshape(local_heads, ATTENTION_SPAN)
    bias_local = lax.dynamic_slice_in_dim(
        cluster_mean_shift_add, feature_start, partition_extent, 0
    ).reshape(local_heads, ATTENTION_SPAN)
    blocked = (stretches, CH, local_heads, ATTENTION_SPAN)
    request_vectors = query_head.reshape(blocked).astype(jnp.float32)
    lookup_vectors = key_head.reshape(blocked).astype(jnp.float32)
    payload_vectors = value_head.reshape(blocked).astype(jnp.float32)
    decays = decay_head.reshape(blocked).astype(jnp.float32)
    cumulative = jnp.cumsum(decays, axis=1)
    before = cumulative - decays
    ending = cumulative[:, -1]
    scaled_query = request_vectors * jnp.exp(before)
    scaled_key = lookup_vectors * jnp.exp(-cumulative)
    scores = jnp.einsum("cthd,cshd->chts", scaled_query, scaled_key, precision=highest)
    causal = lax.broadcasted_iota(jnp.int32, (CH, CH), 0) > lax.broadcasted_iota(
        jnp.int32, (CH, CH), 1
    )
    allowed = causal[None] & (seg_block[:, :, None] == seg_block[:, None, :])
    scores = jnp.where(allowed[:, None], scores, jnp.zeros_like(scores))
    within = jnp.einsum("chts,cshd->cthd", scores, payload_vectors, precision=highest)
    diagonal_contribution = (
        jnp.sum(request_vectors * partition_reward * lookup_vectors, axis=3, keepdims=True)
        * payload_vectors
    )
    keep_last = (seg_block == seg_block[:, -1:]).astype(jnp.float32)
    tail_keys = lookup_vectors * jnp.exp(ending[:, None] - cumulative) * keep_last[:, :, None, None]
    stretch_state = jnp.einsum("cthd,cthe->chde", tail_keys, payload_vectors, precision=highest)
    stretch_decay = (
        jnp.exp(ending) * (seg_block[:, -1] == stretch_prior).astype(jnp.float32)[:, None, None]
    )

    zero_state = jnp.zeros((local_heads, ATTENTION_SPAN, ATTENTION_SPAN), jnp.float32)
    span_state = zero_state
    span_decay = jnp.ones((local_heads, ATTENTION_SPAN), jnp.float32)
    starts, decays_before = [], []
    for stretch in range(stretches):
        starts.append(span_state)
        decays_before.append(span_decay)
        span_state = stretch_decay[stretch][:, :, None] * span_state + stretch_state[stretch]
        span_decay = span_decay * stretch_decay[stretch]
    local_start = jnp.stack(starts)
    decay_before = jnp.stack(decays_before)

    def fold(gathered, position):
        count = gathered.shape[0]
        prefix_state = jnp.zeros_like(gathered[0, :, :ATTENTION_SPAN])
        prefix_decay = jnp.ones_like(gathered[0, :, ATTENTION_SPAN])
        total_state, total_decay = prefix_state, prefix_decay
        for k in range(count):
            part_decay = gathered[k, :, ATTENTION_SPAN]
            part_state = gathered[k, :, :ATTENTION_SPAN]
            take = k < position
            prefix_state = jnp.where(
                take, part_decay[:, :, None] * prefix_state + part_state, prefix_state
            )
            prefix_decay = jnp.where(take, part_decay * prefix_decay, prefix_decay)
            total_state = part_decay[:, :, None] * total_state + part_state
            total_decay = part_decay * total_decay
        return (
            jnp.concatenate([prefix_state, prefix_decay[:, None, :]], axis=1),
            jnp.concatenate([total_state, total_decay[:, None, :]], axis=1),
        )

    own = jnp.concatenate([span_state, span_decay[:, None, :]], axis=1)
    core_index = lax.axis_index("core")
    core_count = lax.axis_size("core")
    core_prefix, core_total = fold(lax.all_gather(own, "core"), core_index)
    share = local_heads // core_count
    level_prefixes = []
    running = lax.dynamic_slice_in_dim(core_total, core_index * share, share, 0)
    for axis in ("zl", "zh", "x"):
        position = lax.axis_index(axis)
        if lax.axis_size(axis) == 2:
            partner = lax.ppermute(running, axis, [(0, 1), (1, 0)])
            gathered = jnp.where(
                position == 0, jnp.stack([running, partner]), jnp.stack([partner, running])
            )
        else:
            gathered = lax.all_gather(running, axis)
        prefix, running = fold(gathered, position)
        level_prefixes.append(prefix)
    pair_incoming = level_prefixes[-1][:, :ATTENTION_SPAN]
    for prefix in level_prefixes[-2::-1]:
        pair_incoming = (
            prefix[:, ATTENTION_SPAN][:, :, None] * pair_incoming + prefix[:, :ATTENTION_SPAN]
        )
    pair_incoming = lax.all_gather(pair_incoming, "core", tiled=True)
    incoming = (
        core_prefix[:, ATTENTION_SPAN][:, :, None] * pair_incoming
        + core_prefix[:, :ATTENTION_SPAN]
    )
    start_state = local_start + decay_before[:, :, :, None] * incoming[None]
    keep_first = (seg_block == stretch_prior[:, None]).astype(jnp.float32)
    local_part = lax.optimization_barrier(within + diagonal_contribution)
    half = local_heads // 2
    pieces = []
    for low in (0, half):
        heads = slice(low, low + half)
        carried = jnp.einsum(
            "cthd,chde->cthe",
            scaled_query[:, :, heads] * keep_first[:, :, None, None],
            start_state[:, heads],
            precision=highest,
        )
        mixing = local_part[:, :, heads] + carried
        center = mixing - jnp.mean(mixing, axis=3, keepdims=True)
        spread = jnp.mean(center * center, axis=3, keepdims=True)
        normed = center * lax.rsqrt(spread + norm_eps) * gain_local[heads] + bias_local[heads]
        normed = normed.astype(jnp.bfloat16).reshape(tokens, half * ATTENTION_SPAN)
        piece = lax.all_to_all(normed, "head", split_axis=0, concat_axis=1, tiled=True)
        pieces.append(piece.reshape(row_count, head_count, half * ATTENTION_SPAN))
    returned = jnp.concatenate(pieces, axis=2).reshape(layer_entries.shape)
    return (returned.astype(jnp.float32) * jax.nn.silu(valve_linear.astype(jnp.float32))).astype(
        jnp.bfloat16
    )


def solution(mesh):
    seq_count, head_count = mesh.devices.shape
    core_count = 2
    z_count = min(8, seq_count // core_count)
    z_low = min(2, z_count)
    fine_mesh = jax.sharding.Mesh(
        mesh.devices.reshape(
            seq_count // (z_count * core_count), z_count // z_low, z_low, core_count, head_count
        ),
        ("x", "zh", "zl", "core", "head"),
    )
    return jax.shard_map(
        local,
        mesh=fine_mesh,
        in_specs=(
            P(("x", "zh", "zl", "core", "head"), None),
            P(("x", "zh", "zl", "core", "head"), None),
            P(("x", "zh", "zl", "core", "head"), None),
            P(("x", "zh", "zl", "core", "head"), None),
            P(("x", "zh", "zl", "core", "head"), None),
            P(),
            P(),
            P(),
            P(),
            P(),
            P(),
            P(),
            P(),
        ),
        out_specs=P(("x", "zh", "zl", "core", "head"), None),
        check_vma=False,
    )
```

```python
import jax
import jax.numpy as jnp
from jax import lax
from jax.sharding import PartitionSpec as P

ATTENTION_SPAN = 64
CH = 128


norm_eps = 0.00064
decay_floor = -0.5
highest = lax.Precision.HIGH


def shifted(value, axis, by):
    size = lax.axis_size(axis)
    pairs = [(i, i + by) for i in range(size) if 0 <= i + by < size]
    return lax.ppermute(value, axis, pairs)


def earlier_segment(prompt_label, position):
    earlier = lax.dynamic_slice_in_dim(prompt_label, jnp.maximum(position - 1, 0), 1, 0)
    return jnp.where(position > 0, earlier, jnp.full_like(earlier, -1))


def local(
    acceptance_linear,
    lookup_linear,
    payload_linear,
    valve_linear,
    layer_entries,
    prompt_label,
    fading_baseline,
    previous_mixing_share,
    fading_lower_map,
    fading_raise_map,
    diagonal_reward,
    cluster_gain_vector,
    cluster_mean_shift_add,
):
    head_count = lax.axis_size("head")
    seq_index = lax.axis_index(("x", "zh", "zl", "core"))
    head_index = lax.axis_index("head")
    row_count = layer_entries.shape[0]
    block_start = (seq_index * head_count + head_index) * row_count
    own_seg = lax.dynamic_slice_in_dim(prompt_label, block_start, row_count, 0)
    prior_seg = jnp.concatenate([earlier_segment(prompt_label, block_start), own_seg[:-1]])
    edge_row = shifted(layer_entries[-1:], ("x", "zh", "zl", "core", "head"), 1)
    prev_rows = jnp.concatenate([edge_row, layer_entries[:-1]], axis=0)
    prev_rows = jnp.where((prior_seg == own_seg)[:, None], prev_rows, jnp.zeros_like(prev_rows))
    current = layer_entries.astype(jnp.float32)
    blended_input = (
        current + (prev_rows.astype(jnp.float32) - current) * previous_mixing_share
    ).astype(jnp.bfloat16)
    decay_hidden_rows = jnp.tanh(
        jnp.dot(blended_input, fading_lower_map, preferred_element_type=jnp.float32)
    ).astype(jnp.bfloat16)
    decay_score = fading_baseline + jnp.dot(
        decay_hidden_rows, fading_raise_map, preferred_element_type=jnp.float32
    )
    log_decay = jnp.maximum(-jnp.exp(decay_score), decay_floor).astype(jnp.bfloat16)
    query_head, key_head, value_head, decay_head = (
        lax.all_to_all(acceptance_linear, "head", split_axis=1, concat_axis=0, tiled=True),
        lax.all_to_all(lookup_linear, "head", split_axis=1, concat_axis=0, tiled=True),
        lax.all_to_all(payload_linear, "head", split_axis=1, concat_axis=0, tiled=True),
        lax.all_to_all(log_decay, "head", split_axis=1, concat_axis=0, tiled=True),
    )
    tokens = query_head.shape[0]
    partition_extent = query_head.shape[1]
    local_heads = partition_extent // ATTENTION_SPAN
    stretches = tokens // CH
    seq_start = seq_index * tokens
    seg_block = lax.dynamic_slice_in_dim(prompt_label, seq_start, tokens, 0).reshape(stretches, CH)
    seg_before = earlier_segment(prompt_label, seq_start)
    stretch_prior = jnp.concatenate([seg_before, seg_block[:-1, -1]])
    feature_start = head_index * partition_extent
    partition_reward = lax.dynamic_slice_in_dim(
        diagonal_reward, feature_start, partition_extent, 0
    ).reshape(local_heads, ATTENTION_SPAN)
    gain_local = lax.dynamic_slice_in_dim(
        cluster_gain_vector, feature_start, partition_extent, 0
    ).reshape(local_heads, ATTENTION_SPAN)
    bias_local = lax.dynamic_slice_in_dim(
        cluster_mean_shift_add, feature_start, partition_extent, 0
    ).reshape(local_heads, ATTENTION_SPAN)
    blocked = (stretches, CH, local_heads, ATTENTION_SPAN)
    request_vectors = query_head.reshape(blocked).astype(jnp.float32)
    lookup_vectors = key_head.reshape(blocked).astype(jnp.float32)
    payload_vectors = value_head.reshape(blocked).astype(jnp.float32)
    decays = decay_head.reshape(blocked).astype(jnp.float32)
    cumulative = jnp.cumsum(decays, axis=1)
    before = cumulative - decays
    ending = cumulative[:, -1]
    query_in, before_in, key_in, cumulative_in = lax.optimization_barrier(
        (request_vectors, before, lookup_vectors, cumulative)
    )
    scaled_query = query_in * jnp.exp(before_in)
    scaled_key = key_in * jnp.exp(-cumulative_in)
    scores = jnp.einsum("cthd,cshd->chts", scaled_query, scaled_key, precision=highest)
    causal = lax.broadcasted_iota(jnp.int32, (CH, CH), 0) > lax.broadcasted_iota(
        jnp.int32, (CH, CH), 1
    )
    allowed = causal[None] & (seg_block[:, :, None] == seg_block[:, None, :])
    scores = jnp.where(allowed[:, None], scores, jnp.zeros_like(scores))
    within = jnp.einsum("chts,cshd->cthd", scores, payload_vectors, precision=highest)
    diagonal_contribution = (
        jnp.sum(request_vectors * partition_reward * lookup_vectors, axis=3, keepdims=True)
        * payload_vectors
    )
    keep_last = (seg_block == seg_block[:, -1:]).astype(jnp.float32)
    tail_keys = lookup_vectors * jnp.exp(ending[:, None] - cumulative) * keep_last[:, :, None, None]
    stretch_state = jnp.einsum("cthd,cthe->chde", tail_keys, payload_vectors, precision=highest)
    stretch_decay = (
        jnp.exp(ending) * (seg_block[:, -1] == stretch_prior).astype(jnp.float32)[:, None, None]
    )

    zero_state = jnp.zeros((local_heads, ATTENTION_SPAN, ATTENTION_SPAN), jnp.float32)
    span_state = zero_state
    span_decay = jnp.ones((local_heads, ATTENTION_SPAN), jnp.float32)
    starts, decays_before = [], []
    for stretch in range(stretches):
        starts.append(span_state)
        decays_before.append(span_decay)
        span_state = stretch_decay[stretch][:, :, None] * span_state + stretch_state[stretch]
        span_decay = span_decay * stretch_decay[stretch]
    local_start = jnp.stack(starts)
    decay_before = jnp.stack(decays_before)

    def fold(gathered, position):
        count = gathered.shape[0]
        prefix_state = jnp.zeros_like(gathered[0, :, :ATTENTION_SPAN])
        prefix_decay = jnp.ones_like(gathered[0, :, ATTENTION_SPAN])
        total_state, total_decay = prefix_state, prefix_decay
        for k in range(count):
            part_decay = gathered[k, :, ATTENTION_SPAN]
            part_state = gathered[k, :, :ATTENTION_SPAN]
            take = k < position
            prefix_state = jnp.where(
                take, part_decay[:, :, None] * prefix_state + part_state, prefix_state
            )
            prefix_decay = jnp.where(take, part_decay * prefix_decay, prefix_decay)
            total_state = part_decay[:, :, None] * total_state + part_state
            total_decay = part_decay * total_decay
        return (
            jnp.concatenate([prefix_state, prefix_decay[:, None, :]], axis=1),
            jnp.concatenate([total_state, total_decay[:, None, :]], axis=1),
        )

    own = jnp.concatenate([span_state, span_decay[:, None, :]], axis=1)
    core_index = lax.axis_index("core")
    core_count = lax.axis_size("core")
    core_prefix, core_total = fold(lax.all_gather(own, "core"), core_index)
    share = local_heads // core_count
    level_prefixes = []
    running = lax.dynamic_slice_in_dim(core_total, core_index * share, share, 0)
    for axis in ("zl", "zh", "x"):
        position = lax.axis_index(axis)
        if lax.axis_size(axis) == 2:
            partner = lax.ppermute(running, axis, [(0, 1), (1, 0)])
            gathered = jnp.where(
                position == 0, jnp.stack([running, partner]), jnp.stack([partner, running])
            )
        else:
            gathered = lax.all_gather(running, axis)
        prefix, running = fold(gathered, position)
        level_prefixes.append(prefix)
    pair_incoming = level_prefixes[-1][:, :ATTENTION_SPAN]
    for prefix in level_prefixes[-2::-1]:
        pair_incoming = (
            prefix[:, ATTENTION_SPAN][:, :, None] * pair_incoming + prefix[:, :ATTENTION_SPAN]
        )
    pair_incoming = lax.all_gather(pair_incoming, "core", tiled=True)
    incoming = (
        core_prefix[:, ATTENTION_SPAN][:, :, None] * pair_incoming
        + core_prefix[:, :ATTENTION_SPAN]
    )
    start_state = local_start + decay_before[:, :, :, None] * incoming[None]
    keep_first = (seg_block == stretch_prior[:, None]).astype(jnp.float32)
    carried = jnp.einsum(
        "cthd,chde->cthe",
        scaled_query * keep_first[:, :, None, None],
        start_state,
        precision=highest,
    )
    local_part = lax.optimization_barrier(within + diagonal_contribution)
    mixing = local_part + carried
    center = mixing - jnp.mean(mixing, axis=3, keepdims=True)
    spread = jnp.mean(center * center, axis=3, keepdims=True)
    normed = center * lax.rsqrt(spread + norm_eps) * gain_local + bias_local
    normed = normed.astype(jnp.bfloat16).reshape(tokens, partition_extent)
    returned = lax.all_to_all(normed, "head", split_axis=0, concat_axis=1, tiled=True)
    return (returned.astype(jnp.float32) * jax.nn.silu(valve_linear.astype(jnp.float32))).astype(
        jnp.bfloat16
    )


def solution(mesh):
    seq_count, head_count = mesh.devices.shape
    core_count = 2
    z_count = min(8, seq_count // core_count)
    z_low = min(2, z_count)
    fine_mesh = jax.sharding.Mesh(
        mesh.devices.reshape(
            seq_count // (z_count * core_count), z_count // z_low, z_low, core_count, head_count
        ),
        ("x", "zh", "zl", "core", "head"),
    )
    return jax.shard_map(
        local,
        mesh=fine_mesh,
        in_specs=(
            P(("x", "zh", "zl", "core", "head"), None),
            P(("x", "zh", "zl", "core", "head"), None),
            P(("x", "zh", "zl", "core", "head"), None),
            P(("x", "zh", "zl", "core", "head"), None),
            P(("x", "zh", "zl", "core", "head"), None),
            P(),
            P(),
            P(),
            P(),
            P(),
            P(),
            P(),
            P(),
        ),
        out_specs=P(("x", "zh", "zl", "core", "head"), None),
        check_vma=False,
    )
```

```python
import jax
import jax.numpy as jnp
from jax import lax
from jax.sharding import PartitionSpec as P

ATTENTION_SPAN = 64
CH = 128


norm_eps = 0.00064
decay_floor = -0.5
highest = lax.Precision.HIGH


def shifted(value, axis, by):
    size = lax.axis_size(axis)
    pairs = [(i, i + by) for i in range(size) if 0 <= i + by < size]
    return lax.ppermute(value, axis, pairs)


def earlier_segment(prompt_label, position):
    earlier = lax.dynamic_slice_in_dim(prompt_label, jnp.maximum(position - 1, 0), 1, 0)
    return jnp.where(position > 0, earlier, jnp.full_like(earlier, -1))


def local(
    acceptance_linear,
    lookup_linear,
    payload_linear,
    valve_linear,
    layer_entries,
    prompt_label,
    fading_baseline,
    previous_mixing_share,
    fading_lower_map,
    fading_raise_map,
    diagonal_reward,
    cluster_gain_vector,
    cluster_mean_shift_add,
):
    head_count = lax.axis_size("head")
    seq_index = lax.axis_index(("x", "zh", "zl", "core"))
    head_index = lax.axis_index("head")
    row_count = layer_entries.shape[0]
    block_start = (seq_index * head_count + head_index) * row_count
    own_seg = lax.dynamic_slice_in_dim(prompt_label, block_start, row_count, 0)
    prior_seg = jnp.concatenate([earlier_segment(prompt_label, block_start), own_seg[:-1]])
    edge_row = shifted(layer_entries[-1:], ("x", "zh", "zl", "core", "head"), 1)
    prev_rows = jnp.concatenate([edge_row, layer_entries[:-1]], axis=0)
    prev_rows = jnp.where((prior_seg == own_seg)[:, None], prev_rows, jnp.zeros_like(prev_rows))
    current = layer_entries.astype(jnp.float32)
    blended_input = (
        current + (prev_rows.astype(jnp.float32) - current) * previous_mixing_share
    ).astype(jnp.bfloat16)
    decay_hidden_rows = jnp.tanh(
        jnp.dot(blended_input, fading_lower_map, preferred_element_type=jnp.float32)
    ).astype(jnp.bfloat16)
    decay_score = fading_baseline + jnp.dot(
        decay_hidden_rows, fading_raise_map, preferred_element_type=jnp.float32
    )
    log_decay = jnp.maximum(-jnp.exp(decay_score), decay_floor).astype(jnp.bfloat16)
    query_head, key_head, value_head, decay_head = (
        lax.all_to_all(acceptance_linear, "head", split_axis=1, concat_axis=0, tiled=True),
        lax.all_to_all(lookup_linear, "head", split_axis=1, concat_axis=0, tiled=True),
        lax.all_to_all(payload_linear, "head", split_axis=1, concat_axis=0, tiled=True),
        lax.all_to_all(log_decay, "head", split_axis=1, concat_axis=0, tiled=True),
    )
    tokens = query_head.shape[0]
    partition_extent = query_head.shape[1]
    local_heads = partition_extent // ATTENTION_SPAN
    stretches = tokens // CH
    seq_start = seq_index * tokens
    seg_block = lax.dynamic_slice_in_dim(prompt_label, seq_start, tokens, 0).reshape(stretches, CH)
    seg_before = earlier_segment(prompt_label, seq_start)
    stretch_prior = jnp.concatenate([seg_before, seg_block[:-1, -1]])
    feature_start = head_index * partition_extent
    partition_reward = lax.dynamic_slice_in_dim(
        diagonal_reward, feature_start, partition_extent, 0
    ).reshape(local_heads, ATTENTION_SPAN)
    gain_local = lax.dynamic_slice_in_dim(
        cluster_gain_vector, feature_start, partition_extent, 0
    ).reshape(local_heads, ATTENTION_SPAN)
    bias_local = lax.dynamic_slice_in_dim(
        cluster_mean_shift_add, feature_start, partition_extent, 0
    ).reshape(local_heads, ATTENTION_SPAN)
    blocked = (stretches, CH, local_heads, ATTENTION_SPAN)
    request_vectors = query_head.reshape(blocked).astype(jnp.float32)
    lookup_vectors = key_head.reshape(blocked).astype(jnp.float32)
    payload_vectors = value_head.reshape(blocked).astype(jnp.float32)
    decays = decay_head.reshape(blocked).astype(jnp.float32)
    cumulative = jnp.cumsum(decays, axis=1)
    before = cumulative - decays
    ending = cumulative[:, -1]
    scaled_query = request_vectors * jnp.exp(before)
    scaled_key = lookup_vectors * jnp.exp(-cumulative)
    scores = jnp.einsum("cthd,cshd->chts", scaled_query, scaled_key, precision=highest)
    causal = lax.broadcasted_iota(jnp.int32, (CH, CH), 0) > lax.broadcasted_iota(
        jnp.int32, (CH, CH), 1
    )
    allowed = causal[None] & (seg_block[:, :, None] == seg_block[:, None, :])
    scores = jnp.where(allowed[:, None], scores, jnp.zeros_like(scores))
    within = jnp.einsum("chts,cshd->cthd", scores, payload_vectors, precision=highest)
    diagonal_contribution = (
        jnp.sum(request_vectors * partition_reward * lookup_vectors, axis=3, keepdims=True)
        * payload_vectors
    )
    keep_last = (seg_block == seg_block[:, -1:]).astype(jnp.float32)
    tail_keys = lookup_vectors * jnp.exp(ending[:, None] - cumulative) * keep_last[:, :, None, None]
    stretch_state = jnp.einsum("cthd,cthe->chde", tail_keys, payload_vectors, precision=highest)
    stretch_decay = (
        jnp.exp(ending) * (seg_block[:, -1] == stretch_prior).astype(jnp.float32)[:, None, None]
    )

    zero_state = jnp.zeros((local_heads, ATTENTION_SPAN, ATTENTION_SPAN), jnp.float32)
    span_state = zero_state
    span_decay = jnp.ones((local_heads, ATTENTION_SPAN), jnp.float32)
    starts, decays_before = [], []
    for stretch in range(stretches):
        starts.append(span_state)
        decays_before.append(span_decay)
        span_state = stretch_decay[stretch][:, :, None] * span_state + stretch_state[stretch]
        span_decay = span_decay * stretch_decay[stretch]
    local_start = jnp.stack(starts)
    decay_before = jnp.stack(decays_before)

    def fold(gathered, position):
        count = gathered.shape[0]
        prefix_state = jnp.zeros_like(gathered[0, :, :ATTENTION_SPAN])
        prefix_decay = jnp.ones_like(gathered[0, :, ATTENTION_SPAN])
        total_state, total_decay = prefix_state, prefix_decay
        for k in range(count):
            part_decay = gathered[k, :, ATTENTION_SPAN]
            part_state = gathered[k, :, :ATTENTION_SPAN]
            take = k < position
            prefix_state = jnp.where(
                take, part_decay[:, :, None] * prefix_state + part_state, prefix_state
            )
            prefix_decay = jnp.where(take, part_decay * prefix_decay, prefix_decay)
            total_state = part_decay[:, :, None] * total_state + part_state
            total_decay = part_decay * total_decay
        return (
            jnp.concatenate([prefix_state, prefix_decay[:, None, :]], axis=1),
            jnp.concatenate([total_state, total_decay[:, None, :]], axis=1),
        )

    own = jnp.concatenate([span_state, span_decay[:, None, :]], axis=1)
    core_index = lax.axis_index("core")
    core_count = lax.axis_size("core")
    core_partner = lax.ppermute(own, "core", [(0, 1), (1, 0)])
    core_pair = jnp.where(
        core_index == 0, jnp.stack([own, core_partner]), jnp.stack([core_partner, own])
    )
    core_prefix, core_total = fold(core_pair, core_index)
    share = local_heads // core_count
    level_prefixes = []
    running = lax.dynamic_slice_in_dim(core_total, core_index * share, share, 0)
    for axis in ("zl", "zh", "x"):
        position = lax.axis_index(axis)
        if lax.axis_size(axis) == 2:
            partner = lax.ppermute(running, axis, [(0, 1), (1, 0)])
            gathered = jnp.where(
                position == 0, jnp.stack([running, partner]), jnp.stack([partner, running])
            )
        else:
            gathered = lax.all_gather(running, axis)
        prefix, running = fold(gathered, position)
        level_prefixes.append(prefix)
    pair_incoming = level_prefixes[-1][:, :ATTENTION_SPAN]
    for prefix in level_prefixes[-2::-1]:
        pair_incoming = (
            prefix[:, ATTENTION_SPAN][:, :, None] * pair_incoming + prefix[:, :ATTENTION_SPAN]
        )
    incoming_partner = lax.ppermute(pair_incoming, "core", [(0, 1), (1, 0)])
    pair_incoming = jnp.where(
        core_index == 0,
        jnp.concatenate([pair_incoming, incoming_partner]),
        jnp.concatenate([incoming_partner, pair_incoming]),
    )
    incoming = (
        core_prefix[:, ATTENTION_SPAN][:, :, None] * pair_incoming
        + core_prefix[:, :ATTENTION_SPAN]
    )
    start_state = local_start + decay_before[:, :, :, None] * incoming[None]
    keep_first = (seg_block == stretch_prior[:, None]).astype(jnp.float32)
    carried = jnp.einsum(
        "cthd,chde->cthe",
        scaled_query * keep_first[:, :, None, None],
        start_state,
        precision=highest,
    )
    local_part = lax.optimization_barrier(within + diagonal_contribution)
    mixing = local_part + carried
    center = mixing - jnp.mean(mixing, axis=3, keepdims=True)
    spread = jnp.mean(center * center, axis=3, keepdims=True)
    normed = center * lax.rsqrt(spread + norm_eps) * gain_local + bias_local
    normed = normed.astype(jnp.bfloat16).reshape(tokens, partition_extent)
    returned = lax.all_to_all(normed, "head", split_axis=0, concat_axis=1, tiled=True)
    return (returned.astype(jnp.float32) * jax.nn.silu(valve_linear.astype(jnp.float32))).astype(
        jnp.bfloat16
    )


def solution(mesh):
    seq_count, head_count = mesh.devices.shape
    core_count = 2
    z_count = min(8, seq_count // core_count)
    z_low = min(2, z_count)
    fine_mesh = jax.sharding.Mesh(
        mesh.devices.reshape(
            seq_count // (z_count * core_count), z_count // z_low, z_low, core_count, head_count
        ),
        ("x", "zh", "zl", "core", "head"),
    )
    return jax.shard_map(
        local,
        mesh=fine_mesh,
        in_specs=(
            P(("x", "zh", "zl", "core", "head"), None),
            P(("x", "zh", "zl", "core", "head"), None),
            P(("x", "zh", "zl", "core", "head"), None),
            P(("x", "zh", "zl", "core", "head"), None),
            P(("x", "zh", "zl", "core", "head"), None),
            P(),
            P(),
            P(),
            P(),
            P(),
            P(),
            P(),
            P(),
        ),
        out_specs=P(("x", "zh", "zl", "core", "head"), None),
        check_vma=False,
    )
```
